256 devices in a mesh: level: 2 (over core), row: 16 (over z_lo, x), col: 8 (over z_hi, y).
Axes of the slice: x: 4, y: 4, z: 8 (z_hi: 2, z_lo: 4; z = z_hi * 4 + z_lo), core: 2. Of those that a mesh axis runs over, the one named last changes fastest.
Arguments:
- friction: float32 [2, 1024, 2048], P('level', 'row', 'col'), may hold values from 0.1 to 4
- height: float32 [2, 1024, 2048], P('level', 'row', 'col'), may hold values from -3 to 3
- inflow: float32 [1024], replicated, may hold values from -2 to 2
Outputs:
- fine_mean: float32 [2, 3, 512, 1024], P('level', None, 'row', 'col')
- correction: float32 [2, 3, 512, 1024], P('level', None, 'row', 'col')
The draws below stay inside these ranges and needn't reach their ends.
All inputs are finite; a program needn't handle non-finite values.
Results may differ from the reference program's by a relative error of at most 0.0003.
Values sent between devices are 32-bit elements; how exact they have to be, the bound alone decides.
No kernel may reach another device: no remote copies, remote signals or barrier semaphores. Data moves between devices by JAX's collectives and lax.ppermute only.
A program may use at most 128 MiB of HBM per device.

```python
import math
import jax
import jax.numpy as jnp
from jax import lax

FR = 64
NXF = 1024
HALF = 2048
N_COL = 8


def shard_levels(rng, shape, split, low, largest):
    def one(dim, shards_of):
        steps = jax.random.uniform(jax.random.fold_in(jax.random.fold_in(rng, 6), dim), (shards_of,), jnp.float32, low / len(split), largest / len(split))
        return jnp.repeat(jnp.exp(steps), shape[dim] // shards_of).reshape((-1,) + (1,) * (len(shape) - dim - 1))

    loudness = one(*split[0])
    for cut in split[1:]:
        loudness = loudness * one(*cut)
    return loudness


def scatter_about(rng, extent, scale, reach, split=(), held_as=jnp.bfloat16):
    array = jax.random.normal(rng, extent, jnp.float32) * scale
    if len(split) > 0:
        array = shard_levels(rng, extent, split, -0.22, 0.18) * array
    return jnp.clip(array, min=-reach, max=reach).astype(held_as)


def setup_inputs(seed: int = 0) -> dict:
    key_of = jax.random.split(jax.random.key(seed), 4)
    friction = jnp.clip(jnp.exp(math.log(4.0) - 3.6888794 * jax.random.uniform(key_of[0], (2, NXF, HALF), jnp.float32) ** shard_levels(key_of[0], (2, NXF, HALF), ((0, 2), (1, 16), (2, 8)), -0.2, 0.2)), 0.1, 4.0)
    height = scatter_about(key_of[1], (2, NXF, HALF), 1.0, 3.0, ((0, 2), (1, 16), (2, 8)), jnp.float32)
    inflow = scatter_about(key_of[2], (NXF,), 0.5, 2.0, (), jnp.float32)
    return {"friction": friction, "height": height, "inflow": inflow}


step_ratio = 0.15

def restrict(values):
    lead = values.shape[:-2]
    count_rows, count_cols = (values.shape[-2], values.shape[-1])
    blocks = values.reshape(lead + (count_rows // 2, 2, count_cols // 2, 2))
    return (blocks[..., 0, :, 0] + blocks[..., 1, :, 0] + blocks[..., 0, :, 1] + blocks[..., 1, :, 1]) * 0.25

def pair_mean(values):
    paired = values.reshape(-1, 2)
    return (paired[:, 0] + paired[:, 1]) * 0.5

def apply_walls(padded, layer, at_top, at_bottom, at_left, at_right, inflow_speed):
    count_rows = padded.shape[1]
    count_cols = padded.shape[2]
    source = padded[:, layer + 1, :]
    mirror = jnp.stack([source[0], source[1], -source[2]])
    padded = padded.at[:, layer, :].set(jnp.where(at_top, mirror, padded[:, layer, :]))
    source = padded[:, count_rows - 2 - layer, :]
    mirror = jnp.stack([source[0], source[1], -source[2]])
    padded = padded.at[:, count_rows - 1 - layer, :].set(jnp.where(at_bottom, mirror, padded[:, count_rows - 1 - layer, :]))
    source = padded[:, :, layer + 1]
    entering = jnp.stack([source[0], source[0] * inflow_speed, jnp.zeros_like(source[0])])
    padded = padded.at[:, :, layer].set(jnp.where(at_left, entering, padded[:, :, layer]))
    padded = padded.at[:, :, count_cols - 1 - layer].set(jnp.where(at_right, padded[:, :, count_cols - 2 - layer], padded[:, :, count_cols - 1 - layer]))
    return padded

def advance(padded, friction_coef, step):
    across = padded[:, 1:-1, :]
    depth = across[0]
    velocity = across[1] / depth
    flux = jnp.stack([across[1], across[1] * velocity + 0.5 * depth * depth, across[2] * velocity])
    speed = jnp.abs(velocity) + jnp.sqrt(depth)
    face_x = 0.5 * (flux[:, :, 1:] + flux[:, :, :-1]) - 0.5 * jnp.maximum(speed[:, 1:], speed[:, :-1]) * (across[:, :, 1:] - across[:, :, :-1])
    along = padded[:, :, 1:-1]
    depth = along[0]
    velocity = along[2] / depth
    flux = jnp.stack([along[2], along[1] * velocity, along[2] * velocity + 0.5 * depth * depth])
    speed = jnp.abs(velocity) + jnp.sqrt(depth)
    face_y = 0.5 * (flux[:, 1:, :] + flux[:, :-1, :]) - 0.5 * jnp.maximum(speed[1:, :], speed[:-1, :]) * (along[:, 1:, :] - along[:, :-1, :])
    moved = padded[:, 1:-1, 1:-1] - step_ratio * (face_x[:, :, 1:] - face_x[:, :, :-1] + (face_y[:, 1:, :] - face_y[:, :-1, :]))
    depth = moved[0]
    speed = jnp.sqrt(moved[1] * moved[1] + moved[2] * moved[2]) / depth
    damping = 1.0 / (1.0 + step * friction_coef * speed / depth)
    return jnp.stack([depth, moved[1] * damping, moved[2] * damping])

def sweep_level(state, friction_coef, step, inflow_speed, block_rows):
    padded = jnp.pad(state, ((0, 0), (1, 1), (1, 1)))
    padded = apply_walls(padded, 0, True, True, True, True, inflow_speed)
    total_rows = state.shape[1]
    total_cols = state.shape[2]
    count_blocks = total_rows // block_rows

    def one_block(block_index):
        start = (block_index * block_rows).astype(jnp.int32)
        piece = lax.dynamic_slice_in_dim(padded, start, block_rows + 2, 1)
        coef_piece = lax.dynamic_slice_in_dim(friction_coef, start, block_rows, 0)
        return advance(piece, coef_piece, step)
    blocks = lax.map(one_block, jnp.arange(count_blocks, dtype=jnp.int32))
    return blocks.transpose(1, 0, 2, 3).reshape(3, total_rows, total_cols)

def unfold(halves):
    total_rows = halves.shape[1]
    tile_half = halves.shape[2] // N_COL
    return halves.reshape(2, total_rows, N_COL, tile_half).transpose(1, 2, 0, 3).reshape(total_rows, 2 * halves.shape[2])

def fold(field):
    total_rows = field.shape[1]
    quarter = field.shape[2] // (2 * N_COL)
    return field.reshape(3, total_rows, N_COL, 2, quarter).transpose(3, 0, 1, 2, 4).reshape(2, 3, total_rows, N_COL * quarter)

def reference(friction, height, inflow):
    fine_coef = unfold(friction)
    noise_fine = unfold(height)
    depth = 1.0 + 0.1 * noise_fine
    fine_state = jnp.stack([depth, 0.5 * depth, jnp.zeros_like(depth)])
    coarse_coef = restrict(fine_coef)
    depth_coarse = 1.0 + 0.1 * restrict(noise_fine)
    coarse_state = jnp.stack([depth_coarse, 0.5 * depth_coarse, jnp.zeros_like(depth_coarse)])
    fine_inflow = 0.5 + jnp.pad(inflow, 1)
    coarse_inflow = 0.5 + jnp.pad(pair_mean(inflow), 1)
    for turn_index in range(2):
        fine_state = sweep_level(fine_state, fine_coef, 0.15, fine_inflow, FR)
    coarse_state = sweep_level(coarse_state, coarse_coef, 0.3, coarse_inflow, FR // 2)
    fine_avg = restrict(fine_state)
    return (fold(fine_avg), fold(fine_avg - coarse_state))
```

```python
import jax
import jax.numpy as jnp
from jax import lax
from jax.sharding import PartitionSpec as P

step_ratio = 0.15
fine_step = 0.15
coarse_step = 0.3
HALO = 2


def shift_pairs(count, delta, place=lambda i: i):
    return [(place(i), place(i + delta)) for i in range(count) if 0 <= i + delta < count]


def strip_place(strip):
    levels = lax.axis_size("level")
    return (strip % levels) * lax.axis_size("col") + strip // levels


def pair_matrix(count):
    rows = jnp.arange(count)[:, None] // 2
    cols = jnp.arange(count // 2)[None, :]
    return (rows == cols).astype(jnp.float32)


def restrict(values):
    lead = values.shape[:-2]
    count_rows, count_cols = values.shape[-2], values.shape[-1]
    rows = values.reshape(lead + (count_rows // 2, 2, count_cols))
    rows = rows[..., 0, :] + rows[..., 1, :]
    both = jnp.einsum(
        "...ij,jk->...ik", rows, pair_matrix(count_cols), precision=lax.Precision.HIGHEST
    )
    return both * 0.25


def pair_mean(values):
    paired = values.reshape(-1, 2)
    return (paired[:, 0] + paired[:, 1]) * 0.5


def apply_walls(padded, layer, at_top, at_bottom, at_left, at_right, inflow_speed):
    count_rows = padded.shape[1]
    count_cols = padded.shape[2]
    low = count_rows - 1 - layer
    source = padded[:, layer + 1, :]
    mirror = jnp.stack([source[0], source[1], -source[2]])
    top = jnp.where(at_top, mirror, padded[:, layer, :])
    source = padded[:, low - 1, :]
    mirror = jnp.stack([source[0], source[1], -source[2]])
    bottom = jnp.where(at_bottom, mirror, padded[:, low, :])
    padded = jnp.concatenate(
        [padded[:, :layer], top[:, None], padded[:, layer + 1: low], bottom[:, None],
         padded[:, low + 1:]],
        axis=1,
    )
    right_col = count_cols - 1 - layer
    source = padded[:, :, layer + 1]
    entering = jnp.stack([source[0], source[0] * inflow_speed, jnp.zeros_like(source[0])])
    left = jnp.where(at_left, entering, padded[:, :, layer])
    right = jnp.where(at_right, padded[:, :, right_col - 1], padded[:, :, right_col])
    return jnp.concatenate(
        [padded[:, :, :layer], left[:, :, None], padded[:, :, layer + 1: right_col],
         right[:, :, None], padded[:, :, right_col + 1:]],
        axis=2,
    )


def advance(padded, friction_coef, step):
    across = padded[:, 1:-1, :]
    depth = across[0]
    velocity = across[1] / depth
    flux = jnp.stack([across[1], across[1] * velocity + 0.5 * depth * depth, across[2] * velocity])
    speed = jnp.abs(velocity) + jnp.sqrt(depth)
    face_x = 0.5 * (flux[:, :, 1:] + flux[:, :, :-1]) - 0.5 * jnp.maximum(
        speed[:, 1:], speed[:, :-1]
    ) * (across[:, :, 1:] - across[:, :, :-1])
    along = padded[:, :, 1:-1]
    depth = along[0]
    velocity = along[2] / depth
    flux = jnp.stack([along[2], along[1] * velocity, along[2] * velocity + 0.5 * depth * depth])
    speed = jnp.abs(velocity) + jnp.sqrt(depth)
    face_y = 0.5 * (flux[:, 1:, :] + flux[:, :-1, :]) - 0.5 * jnp.maximum(
        speed[1:, :], speed[:-1, :]
    ) * (along[:, 1:, :] - along[:, :-1, :])
    moved = padded[:, 1:-1, 1:-1] - step_ratio * (
        face_x[:, :, 1:] - face_x[:, :, :-1] + (face_y[:, 1:, :] - face_y[:, :-1, :])
    )
    depth = moved[0]
    speed = jnp.sqrt(moved[1] * moved[1] + moved[2] * moved[2]) / depth
    damping = 1.0 / (1.0 + step * friction_coef * speed / depth)
    return jnp.stack([depth, moved[1] * damping, moved[2] * damping])


def with_halo(noise):
    strips = lax.axis_size("col") * lax.axis_size("level")
    rows = lax.axis_size("row")
    across = ("level", "col")
    west = lax.ppermute(noise[:, :, -HALO:], across, shift_pairs(strips, 1, strip_place))
    east = lax.ppermute(noise[:, :, :HALO], across, shift_pairs(strips, -1, strip_place))
    wide = jnp.concatenate([west, noise, east], axis=2)
    north = lax.ppermute(wide[:, -HALO:, :], "row", shift_pairs(rows, 1))
    south = lax.ppermute(wide[:, :HALO, :], "row", shift_pairs(rows, -1))
    return jnp.concatenate([north, wide, south], axis=1)


def body(friction, height, inflow):
    strip = lax.axis_index("col") * lax.axis_size("level") + lax.axis_index("level")
    strips = lax.axis_size("col") * lax.axis_size("level")
    row_index = lax.axis_index("row")
    at_top = row_index == 0
    at_bottom = row_index == lax.axis_size("row") - 1
    at_left = strip == 0
    at_right = strip == strips - 1
    tile_rows = friction.shape[1]
    coarse_rows = tile_rows // 2

    noise = with_halo(jnp.concatenate([friction, height], axis=0))
    fine_coef = noise[0]
    depth = 1.0 + 0.1 * noise[1]
    state = jnp.stack([depth, 0.5 * depth, jnp.zeros_like(depth)])

    fine_inflow = 0.5 + lax.dynamic_slice_in_dim(
        jnp.pad(inflow, HALO), row_index * tile_rows, tile_rows + 2 * HALO
    )
    for turn_index in range(2):
        padded = apply_walls(
            state, HALO - 1 - turn_index, at_top, at_bottom, at_left, at_right,
            fine_inflow[turn_index: fine_inflow.shape[0] - turn_index],
        )
        inner = turn_index + 1
        coef = fine_coef[inner: fine_coef.shape[0] - inner, inner: fine_coef.shape[1] - inner]
        state = advance(padded, coef, fine_step)

    small = restrict(noise)
    coarse_coef = small[0, 1:-1, 1:-1]
    depth_coarse = 1.0 + 0.1 * small[1]
    coarse_state = jnp.stack([depth_coarse, 0.5 * depth_coarse, jnp.zeros_like(depth_coarse)])
    coarse_inflow = 0.5 + lax.dynamic_slice_in_dim(
        jnp.pad(pair_mean(inflow), 1), row_index * coarse_rows, coarse_rows + 2
    )
    padded = apply_walls(coarse_state, 0, at_top, at_bottom, at_left, at_right, coarse_inflow)
    coarse_state = advance(padded, coarse_coef, coarse_step)

    fine_mean = restrict(state)
    return (fine_mean[None], (fine_mean - coarse_state)[None])


def solution(mesh):
    in_specs = (P("level", "row", "col"), P("level", "row", "col"), P())
    out_specs = (P("level", None, "row", "col"), P("level", None, "row", "col"))
    return jax.shard_map(body, mesh=mesh, in_specs=in_specs, out_specs=out_specs, check_vma=False)
```

```python
import jax
import jax.numpy as jnp
from jax import lax
from jax.experimental import pallas as pl
from jax.experimental.pallas import tpu as pltpu
from jax.sharding import PartitionSpec as P

step_ratio = 0.15
fine_step = 0.15
coarse_step = 0.3
HALO = 2
FINE_SHAPE = (72, 384)
COARSE_SHAPE = (40, 256)


def shift_pairs(count, delta, place=lambda i: i):
    return [(place(i), place(i + delta)) for i in range(count) if 0 <= i + delta < count]


def strip_place(strip):
    levels = lax.axis_size("level")
    return (strip % levels) * lax.axis_size("col") + strip // levels


def pair_mean(values):
    paired = values.reshape(-1, 2)
    return (paired[:, 0] + paired[:, 1]) * 0.5


def with_halo(noise):
    fields, count_rows, count_cols = noise.shape
    strips = lax.axis_size("col") * lax.axis_size("level")
    rows = lax.axis_size("row")
    across = ("level", "col")
    west = lax.ppermute(noise[:, :, -HALO:], across, shift_pairs(strips, 1, strip_place))
    east = lax.ppermute(noise[:, :, :HALO], across, shift_pairs(strips, -1, strip_place))
    gap_cols = FINE_SHAPE[1] - count_cols - 2 * HALO
    wide = jnp.concatenate(
        [noise, east, jnp.zeros((fields, count_rows, gap_cols), noise.dtype), west], axis=2
    )
    north = lax.ppermute(wide[:, -HALO:, :], "row", shift_pairs(rows, 1))
    south = lax.ppermute(wide[:, :HALO, :], "row", shift_pairs(rows, -1))
    gap_rows = FINE_SHAPE[0] - count_rows - 2 * HALO
    return jnp.concatenate(
        [wide, south, jnp.zeros((fields, gap_rows, FINE_SHAPE[1]), noise.dtype), north], axis=1
    )


def wrapped_rows(values, start, count, lead):
    padded = jnp.pad(values, lead)
    window = lax.dynamic_slice_in_dim(padded, start, count)
    return (0.5 + jnp.roll(window, -lead)).reshape(count, 1)


def next_of(values, axis):
    return pltpu.roll(values, values.shape[axis] - 1, axis)


def prev_of(values, axis):
    return pltpu.roll(values, 1, axis)


def apply_walls(state, flags, inflow_speed, bottom_row, right_col):
    depth, along_cols, along_rows = state
    shape = depth.shape
    row_at = lax.broadcasted_iota(jnp.int32, shape, 0)
    col_at = lax.broadcasted_iota(jnp.int32, shape, 1)
    top = jnp.logical_and(row_at == shape[0] - 1, flags[0] == 1)
    bottom = jnp.logical_and(row_at == bottom_row, flags[1] == 1)
    left = jnp.logical_and(col_at == shape[1] - 1, flags[2] == 1)
    right = jnp.logical_and(col_at == right_col, flags[3] == 1)

    def rows_fixed(values, sign):
        below = next_of(values, 0)
        above = prev_of(values, 0)
        if sign < 0:
            below = -below
            above = -above
        return jnp.where(top, below, jnp.where(bottom, above, values))

    depth = rows_fixed(depth, 1)
    along_cols = rows_fixed(along_cols, 1)
    along_rows = rows_fixed(along_rows, -1)
    source = next_of(depth, 1)
    entering = (source, source * inflow_speed, jnp.zeros_like(source))
    fixed = []
    for values, inflowing in zip((depth, along_cols, along_rows), entering):
        fixed.append(jnp.where(left, inflowing, jnp.where(right, prev_of(values, 1), values)))
    return tuple(fixed)


def face_flux(state, flux, speed, axis):
    reach = 0.5 * jnp.maximum(next_of(speed, axis), speed)
    return [
        0.5 * (next_of(f, axis) + f) - reach * (next_of(u, axis) - u)
        for f, u in zip(flux, state)
    ]


def advance(state, friction_coef, step):
    depth, along_cols, along_rows = state
    velocity = along_cols / depth
    flux = (along_cols, along_cols * velocity + 0.5 * depth * depth, along_rows * velocity)
    face_x = face_flux(state, flux, jnp.abs(velocity) + jnp.sqrt(depth), 1)
    velocity = along_rows / depth
    flux = (along_rows, along_cols * velocity, along_rows * velocity + 0.5 * depth * depth)
    face_y = face_flux(state, flux, jnp.abs(velocity) + jnp.sqrt(depth), 0)
    moved = [
        u - step_ratio * (fx - prev_of(fx, 1) + (fy - prev_of(fy, 0)))
        for u, fx, fy in zip(state, face_x, face_y)
    ]
    depth = moved[0]
    speed = jnp.sqrt(moved[1] * moved[1] + moved[2] * moved[2]) / depth
    damping = 1.0 / (1.0 + step * friction_coef * speed / depth)
    return (depth, moved[1] * damping, moved[2] * damping)


def pair_matrix(shape, out_axis, last_from):
    out_at = lax.broadcasted_iota(jnp.int32, shape, out_axis)
    in_at = lax.broadcasted_iota(jnp.int32, shape, 1 - out_axis)
    hit = jnp.right_shift(in_at, 1) == out_at
    if last_from is not None:
        last = shape[out_axis] - 1
        hit = jnp.logical_or(hit, jnp.logical_and(out_at == last, in_at >= last_from))
    return hit.astype(jnp.float32)


def matmul(a, b):
    return jnp.dot(a, b, precision=lax.Precision.HIGHEST, preferred_element_type=jnp.float32)


def level_kernel(flags_ref, noise_ref, fine_inflow_ref, coarse_inflow_ref, mean_ref, corr_ref):
    flags = [flags_ref[i] for i in range(4)]
    fine_rows, fine_cols = FINE_SHAPE
    coarse_rows, coarse_cols = COARSE_SHAPE
    out_rows, out_cols = mean_ref.shape[1], mean_ref.shape[2]
    tile_rows, tile_cols = 2 * out_rows, 2 * out_cols

    fine_coef = noise_ref[0]
    noise_height = noise_ref[1]
    depth = 1.0 + 0.1 * noise_height
    state = (depth, 0.5 * depth, jnp.zeros_like(depth))
    fine_inflow = jnp.broadcast_to(fine_inflow_ref[...], FINE_SHAPE)
    for _ in range(2):
        state = apply_walls(state, flags, fine_inflow, tile_rows, tile_cols)
        state = advance(state, fine_coef, fine_step)

    rows_sum = pair_matrix((coarse_rows, fine_rows), 0, fine_rows - 2)
    cols_sum = pair_matrix((fine_cols, coarse_cols), 1, fine_cols - 2)
    coarse_coef = matmul(matmul(rows_sum, fine_coef), cols_sum) * 0.25
    depth = 1.0 + 0.1 * (matmul(matmul(rows_sum, noise_height), cols_sum) * 0.25)
    coarse = (depth, 0.5 * depth, jnp.zeros_like(depth))
    coarse_inflow = jnp.broadcast_to(coarse_inflow_ref[...], COARSE_SHAPE)
    coarse = apply_walls(coarse, flags, coarse_inflow, out_rows, out_cols)
    coarse = advance(coarse, coarse_coef, coarse_step)

    rows_out = pair_matrix((out_rows, tile_rows), 0, None)
    cols_out = pair_matrix((tile_cols, out_cols), 1, None)
    for field in range(3):
        fine_part = state[field][:tile_rows, :tile_cols]
        mean = matmul(matmul(rows_out, fine_part), cols_out) * 0.25
        mean_ref[field] = mean
        corr_ref[field] = mean - coarse[field][:out_rows, :out_cols]


def body(friction, height, inflow):
    strip = lax.axis_index("col") * lax.axis_size("level") + lax.axis_index("level")
    strips = lax.axis_size("col") * lax.axis_size("level")
    row_index = lax.axis_index("row")
    flags = jnp.stack(
        [row_index == 0, row_index == lax.axis_size("row") - 1, strip == 0, strip == strips - 1]
    ).astype(jnp.int32)
    tile_rows, tile_cols = friction.shape[1], friction.shape[2]
    out_rows, out_cols = tile_rows // 2, tile_cols // 2

    noise = with_halo(jnp.concatenate([friction, height], axis=0))
    lead = FINE_SHAPE[0] - tile_rows - HALO
    fine_inflow = wrapped_rows(inflow, row_index * tile_rows, FINE_SHAPE[0], lead)
    lead = COARSE_SHAPE[0] - out_rows - 1
    coarse_inflow = wrapped_rows(pair_mean(inflow), row_index * out_rows, COARSE_SHAPE[0], lead)

    out = jax.ShapeDtypeStruct((3, out_rows, out_cols), jnp.float32)
    vmem = pl.BlockSpec(memory_space=pltpu.VMEM)
    mean, corr = pl.pallas_call(
        level_kernel,
        out_shape=(out, out),
        in_specs=[pl.BlockSpec(memory_space=pltpu.SMEM), vmem, vmem, vmem],
        out_specs=(vmem, vmem),
    )(flags, noise, fine_inflow, coarse_inflow)
    return (mean[None], corr[None])


def solution(mesh):
    in_specs = (P("level", "row", "col"), P("level", "row", "col"), P())
    out_specs = (P("level", None, "row", "col"), P("level", None, "row", "col"))
    return jax.shard_map(body, mesh=mesh, in_specs=in_specs, out_specs=out_specs, check_vma=False)
```

```python
import jax
import jax.numpy as jnp
from jax import lax
from jax.experimental import pallas as pl
from jax.experimental.pallas import tpu as pltpu
from jax.sharding import PartitionSpec as P

step_ratio = 0.15
fine_step = 0.15
coarse_step = 0.3
HALO = 2
FINE_SHAPE = (72, 384)
COARSE_SHAPE = (40, 256)


def pair_mean(values):
    paired = values.reshape(-1, 2)
    return (paired[:, 0] + paired[:, 1]) * 0.5


def with_halo(noise):
    fields, count_rows, count_cols = noise.shape
    levels, cols, rows = lax.axis_size("level"), lax.axis_size("col"), lax.axis_size("row")
    strips = levels * cols

    def place(row, strip):
        return ((strip % levels) * rows + row) * cols + strip // levels

    def sent(block, down, right):
        pairs = [
            (place(r, s), place(r + down, s + right))
            for r in range(rows) for s in range(strips)
            if 0 <= r + down < rows and 0 <= s + right < strips
        ]
        return lax.ppermute(block, ("level", "row", "col"), pairs)

    top, low = slice(0, HALO), slice(count_rows - HALO, count_rows)
    first, last = slice(0, HALO), slice(count_cols - HALO, count_cols)
    west = sent(noise[:, :, last], 0, 1)
    east = sent(noise[:, :, first], 0, -1)
    north = sent(noise[:, low, :], 1, 0)
    south = sent(noise[:, top, :], -1, 0)
    north_west = sent(noise[:, low, last], 1, 1)
    north_east = sent(noise[:, low, first], 1, -1)
    south_west = sent(noise[:, top, last], -1, 1)
    south_east = sent(noise[:, top, first], -1, -1)
    gap_cols = FINE_SHAPE[1] - count_cols - 2 * HALO

    def band(middle, after, before):
        gap = jnp.zeros(middle.shape[:2] + (gap_cols,), noise.dtype)
        return jnp.concatenate([middle, after, gap, before], axis=2)

    gap_rows = FINE_SHAPE[0] - count_rows - 2 * HALO
    return jnp.concatenate(
        [
            band(noise, east, west),
            band(south, south_east, south_west),
            jnp.zeros((fields, gap_rows, FINE_SHAPE[1]), noise.dtype),
            band(north, north_east, north_west),
        ],
        axis=1,
    )


def wrapped_rows(values, start, count, lead):
    padded = jnp.pad(values, lead)
    window = lax.dynamic_slice_in_dim(padded, start, count)
    return (0.5 + jnp.roll(window, -lead)).reshape(count, 1)


def next_of(values, axis):
    return pltpu.roll(values, values.shape[axis] - 1, axis)


def prev_of(values, axis):
    return pltpu.roll(values, 1, axis)


def apply_walls(state, flags, inflow_speed, bottom_row, right_col):
    depth, along_cols, along_rows = state
    shape = depth.shape
    row_at = lax.broadcasted_iota(jnp.int32, shape, 0)
    col_at = lax.broadcasted_iota(jnp.int32, shape, 1)
    top = jnp.logical_and(row_at == shape[0] - 1, flags[0] == 1)
    bottom = jnp.logical_and(row_at == bottom_row, flags[1] == 1)
    left = jnp.logical_and(col_at == shape[1] - 1, flags[2] == 1)
    right = jnp.logical_and(col_at == right_col, flags[3] == 1)

    def rows_fixed(values, sign):
        below = next_of(values, 0)
        above = prev_of(values, 0)
        if sign < 0:
            below = -below
            above = -above
        return jnp.where(top, below, jnp.where(bottom, above, values))

    depth = rows_fixed(depth, 1)
    along_cols = rows_fixed(along_cols, 1)
    along_rows = rows_fixed(along_rows, -1)
    source = next_of(depth, 1)
    entering = (source, source * inflow_speed, jnp.zeros_like(source))
    fixed = []
    for values, inflowing in zip((depth, along_cols, along_rows), entering):
        fixed.append(jnp.where(left, inflowing, jnp.where(right, prev_of(values, 1), values)))
    return tuple(fixed)


def face_flux(state, flux, speed, axis):
    reach = 0.5 * jnp.maximum(next_of(speed, axis), speed)
    return [
        0.5 * (next_of(f, axis) + f) - reach * (next_of(u, axis) - u)
        for f, u in zip(flux, state)
    ]


def advance(state, friction_coef, step):
    depth, along_cols, along_rows = state
    velocity = along_cols / depth
    flux = (along_cols, along_cols * velocity + 0.5 * depth * depth, along_rows * velocity)
    face_x = face_flux(state, flux, jnp.abs(velocity) + jnp.sqrt(depth), 1)
    velocity = along_rows / depth
    flux = (along_rows, along_cols * velocity, along_rows * velocity + 0.5 * depth * depth)
    face_y = face_flux(state, flux, jnp.abs(velocity) + jnp.sqrt(depth), 0)
    moved = [
        u - step_ratio * (fx - prev_of(fx, 1) + (fy - prev_of(fy, 0)))
        for u, fx, fy in zip(state, face_x, face_y)
    ]
    depth = moved[0]
    speed = jnp.sqrt(moved[1] * moved[1] + moved[2] * moved[2]) / depth
    damping = 1.0 / (1.0 + step * friction_coef * speed / depth)
    return (depth, moved[1] * damping, moved[2] * damping)


def pair_matrix(shape, out_axis, last_from):
    out_at = lax.broadcasted_iota(jnp.int32, shape, out_axis)
    in_at = lax.broadcasted_iota(jnp.int32, shape, 1 - out_axis)
    hit = jnp.right_shift(in_at, 1) == out_at
    if last_from is not None:
        last = shape[out_axis] - 1
        hit = jnp.logical_or(hit, jnp.logical_and(out_at == last, in_at >= last_from))
    return hit.astype(jnp.float32)


def matmul(a, b):
    return jnp.dot(a, b, precision=lax.Precision.HIGHEST, preferred_element_type=jnp.float32)


def level_kernel(flags_ref, noise_ref, fine_inflow_ref, coarse_inflow_ref, mean_ref, corr_ref):
    flags = [flags_ref[i] for i in range(4)]
    fine_rows, fine_cols = FINE_SHAPE
    coarse_rows, coarse_cols = COARSE_SHAPE
    out_rows, out_cols = mean_ref.shape[1], mean_ref.shape[2]
    tile_rows, tile_cols = 2 * out_rows, 2 * out_cols

    fine_coef = noise_ref[0]
    noise_height = noise_ref[1]
    depth = 1.0 + 0.1 * noise_height
    state = (depth, 0.5 * depth, jnp.zeros_like(depth))
    fine_inflow = jnp.broadcast_to(fine_inflow_ref[...], FINE_SHAPE)
    for _ in range(2):
        state = apply_walls(state, flags, fine_inflow, tile_rows, tile_cols)
        state = advance(state, fine_coef, fine_step)

    rows_sum = pair_matrix((coarse_rows, fine_rows), 0, fine_rows - 2)
    cols_sum = pair_matrix((fine_cols, coarse_cols), 1, fine_cols - 2)
    coarse_coef = matmul(matmul(rows_sum, fine_coef), cols_sum) * 0.25
    depth = 1.0 + 0.1 * (matmul(matmul(rows_sum, noise_height), cols_sum) * 0.25)
    coarse = (depth, 0.5 * depth, jnp.zeros_like(depth))
    coarse_inflow = jnp.broadcast_to(coarse_inflow_ref[...], COARSE_SHAPE)
    coarse = apply_walls(coarse, flags, coarse_inflow, out_rows, out_cols)
    coarse = advance(coarse, coarse_coef, coarse_step)

    rows_out = pair_matrix((out_rows, tile_rows), 0, None)
    cols_out = pair_matrix((tile_cols, out_cols), 1, None)
    for field in range(3):
        fine_part = state[field][:tile_rows, :tile_cols]
        mean = matmul(matmul(rows_out, fine_part), cols_out) * 0.25
        mean_ref[field] = mean
        corr_ref[field] = mean - coarse[field][:out_rows, :out_cols]


def body(friction, height, inflow):
    strip = lax.axis_index("col") * lax.axis_size("level") + lax.axis_index("level")
    strips = lax.axis_size("col") * lax.axis_size("level")
    row_index = lax.axis_index("row")
    flags = jnp.stack(
        [row_index == 0, row_index == lax.axis_size("row") - 1, strip == 0, strip == strips - 1]
    ).astype(jnp.int32)
    tile_rows, tile_cols = friction.shape[1], friction.shape[2]
    out_rows, out_cols = tile_rows // 2, tile_cols // 2

    noise = with_halo(jnp.concatenate([friction, height], axis=0))
    lead = FINE_SHAPE[0] - tile_rows - HALO
    fine_inflow = wrapped_rows(inflow, row_index * tile_rows, FINE_SHAPE[0], lead)
    lead = COARSE_SHAPE[0] - out_rows - 1
    coarse_inflow = wrapped_rows(pair_mean(inflow), row_index * out_rows, COARSE_SHAPE[0], lead)

    out = jax.ShapeDtypeStruct((3, out_rows, out_cols), jnp.float32)
    vmem = pl.BlockSpec(memory_space=pltpu.VMEM)
    mean, corr = pl.pallas_call(
        level_kernel,
        out_shape=(out, out),
        in_specs=[pl.BlockSpec(memory_space=pltpu.SMEM), vmem, vmem, vmem],
        out_specs=(vmem, vmem),
    )(flags, noise, fine_inflow, coarse_inflow)
    return (mean[None], corr[None])


def solution(mesh):
    in_specs = (P("level", "row", "col"), P("level", "row", "col"), P())
    out_specs = (P("level", None, "row", "col"), P("level", None, "row", "col"))
    return jax.shard_map(body, mesh=mesh, in_specs=in_specs, out_specs=out_specs, check_vma=False)
```

```python
import jax
import jax.numpy as jnp
from jax import lax
from jax.experimental import pallas as pl
from jax.experimental.pallas import tpu as pltpu
from jax.sharding import PartitionSpec as P

step_ratio = 0.15
fine_step = 0.15
coarse_step = 0.3
HALO = 2
FINE_SHAPE = (72, 384)
COARSE_SHAPE = (40, 256)


def pair_mean(values):
    paired = values.reshape(-1, 2)
    return (paired[:, 0] + paired[:, 1]) * 0.5


def swap_pairs(count, parity, place=lambda i: i):
    pairs = []
    for i in range(parity, count - 1, 2):
        pairs += [(place(i), place(i + 1)), (place(i + 1), place(i))]
    return pairs


def strip_place(strip):
    levels = lax.axis_size("level")
    return (strip % levels) * lax.axis_size("col") + strip // levels


def swapped(first, last, index, count, axis, place=lambda i: i):
    odd = index % 2 == 1
    got = []
    for parity in range(2):
        sends_last = odd if parity else jnp.logical_not(odd)
        block = jnp.where(sends_last, last, first)
        got.append(lax.ppermute(block, axis, swap_pairs(count, parity, place)))
    before = jnp.where(odd, got[0], got[1])
    after = jnp.where(odd, got[1], got[0])
    return before, after


def with_halo(noise):
    fields, count_rows, count_cols = noise.shape
    strips = lax.axis_size("col") * lax.axis_size("level")
    strip = lax.axis_index("col") * lax.axis_size("level") + lax.axis_index("level")
    rows = lax.axis_size("row")
    west, east = swapped(
        noise[:, :, :HALO], noise[:, :, -HALO:], strip, strips, ("level", "col"), strip_place
    )
    gap_cols = FINE_SHAPE[1] - count_cols - 2 * HALO
    wide = jnp.concatenate(
        [noise, east, jnp.zeros((fields, count_rows, gap_cols), noise.dtype), west], axis=2
    )
    north, south = swapped(wide[:, :HALO], wide[:, -HALO:], lax.axis_index("row"), rows, "row")
    gap_rows = FINE_SHAPE[0] - count_rows - 2 * HALO
    return jnp.concatenate(
        [wide, south, jnp.zeros((fields, gap_rows, FINE_SHAPE[1]), noise.dtype), north], axis=1
    )


def wrapped_rows(values, start, count, lead):
    padded = jnp.pad(values, lead)
    window = lax.dynamic_slice_in_dim(padded, start, count)
    return (0.5 + jnp.roll(window, -lead)).reshape(count, 1)


def next_of(values, axis):
    return pltpu.roll(values, values.shape[axis] - 1, axis)


def prev_of(values, axis):
    return pltpu.roll(values, 1, axis)


def apply_walls(state, flags, inflow_speed, bottom_row, right_col):
    depth, along_cols, along_rows = state
    shape = depth.shape
    row_at = lax.broadcasted_iota(jnp.int32, shape, 0)
    col_at = lax.broadcasted_iota(jnp.int32, shape, 1)
    top = jnp.logical_and(row_at == shape[0] - 1, flags[0] == 1)
    bottom = jnp.logical_and(row_at == bottom_row, flags[1] == 1)
    left = jnp.logical_and(col_at == shape[1] - 1, flags[2] == 1)
    right = jnp.logical_and(col_at == right_col, flags[3] == 1)

    def rows_fixed(values, sign):
        below = next_of(values, 0)
        above = prev_of(values, 0)
        if sign < 0:
            below = -below
            above = -above
        return jnp.where(top, below, jnp.where(bottom, above, values))

    depth = rows_fixed(depth, 1)
    along_cols = rows_fixed(along_cols, 1)
    along_rows = rows_fixed(along_rows, -1)
    source = next_of(depth, 1)
    entering = (source, source * inflow_speed, jnp.zeros_like(source))
    fixed = []
    for values, inflowing in zip((depth, along_cols, along_rows), entering):
        fixed.append(jnp.where(left, inflowing, jnp.where(right, prev_of(values, 1), values)))
    return tuple(fixed)


def face_flux(state, flux, speed, axis):
    reach = 0.5 * jnp.maximum(next_of(speed, axis), speed)
    return [
        0.5 * (next_of(f, axis) + f) - reach * (next_of(u, axis) - u)
        for f, u in zip(flux, state)
    ]


def advance(state, friction_coef, step):
    depth, along_cols, along_rows = state
    velocity = along_cols / depth
    flux = (along_cols, along_cols * velocity + 0.5 * depth * depth, along_rows * velocity)
    face_x = face_flux(state, flux, jnp.abs(velocity) + jnp.sqrt(depth), 1)
    velocity = along_rows / depth
    flux = (along_rows, along_cols * velocity, along_rows * velocity + 0.5 * depth * depth)
    face_y = face_flux(state, flux, jnp.abs(velocity) + jnp.sqrt(depth), 0)
    moved = [
        u - step_ratio * (fx - prev_of(fx, 1) + (fy - prev_of(fy, 0)))
        for u, fx, fy in zip(state, face_x, face_y)
    ]
    depth = moved[0]
    speed = jnp.sqrt(moved[1] * moved[1] + moved[2] * moved[2]) / depth
    damping = 1.0 / (1.0 + step * friction_coef * speed / depth)
    return (depth, moved[1] * damping, moved[2] * damping)


def pair_matrix(shape, out_axis, last_from):
    out_at = lax.broadcasted_iota(jnp.int32, shape, out_axis)
    in_at = lax.broadcasted_iota(jnp.int32, shape, 1 - out_axis)
    hit = jnp.right_shift(in_at, 1) == out_at
    if last_from is not None:
        last = shape[out_axis] - 1
        hit = jnp.logical_or(hit, jnp.logical_and(out_at == last, in_at >= last_from))
    return hit.astype(jnp.float32)


def matmul(a, b):
    return jnp.dot(a, b, precision=lax.Precision.HIGHEST, preferred_element_type=jnp.float32)


def level_kernel(flags_ref, noise_ref, fine_inflow_ref, coarse_inflow_ref, mean_ref, corr_ref):
    flags = [flags_ref[i] for i in range(4)]
    fine_rows, fine_cols = FINE_SHAPE
    coarse_rows, coarse_cols = COARSE_SHAPE
    out_rows, out_cols = mean_ref.shape[1], mean_ref.shape[2]
    tile_rows, tile_cols = 2 * out_rows, 2 * out_cols

    fine_coef = noise_ref[0]
    noise_height = noise_ref[1]
    depth = 1.0 + 0.1 * noise_height
    state = (depth, 0.5 * depth, jnp.zeros_like(depth))
    fine_inflow = jnp.broadcast_to(fine_inflow_ref[...], FINE_SHAPE)
    for _ in range(2):
        state = apply_walls(state, flags, fine_inflow, tile_rows, tile_cols)
        state = advance(state, fine_coef, fine_step)

    rows_sum = pair_matrix((coarse_rows, fine_rows), 0, fine_rows - 2)
    cols_sum = pair_matrix((fine_cols, coarse_cols), 1, fine_cols - 2)
    coarse_coef = matmul(matmul(rows_sum, fine_coef), cols_sum) * 0.25
    depth = 1.0 + 0.1 * (matmul(matmul(rows_sum, noise_height), cols_sum) * 0.25)
    coarse = (depth, 0.5 * depth, jnp.zeros_like(depth))
    coarse_inflow = jnp.broadcast_to(coarse_inflow_ref[...], COARSE_SHAPE)
    coarse = apply_walls(coarse, flags, coarse_inflow, out_rows, out_cols)
    coarse = advance(coarse, coarse_coef, coarse_step)

    rows_out = pair_matrix((out_rows, tile_rows), 0, None)
    cols_out = pair_matrix((tile_cols, out_cols), 1, None)
    for field in range(3):
        fine_part = state[field][:tile_rows, :tile_cols]
        mean = matmul(matmul(rows_out, fine_part), cols_out) * 0.25
        mean_ref[field] = mean
        corr_ref[field] = mean - coarse[field][:out_rows, :out_cols]


def body(friction, height, inflow):
    strip = lax.axis_index("col") * lax.axis_size("level") + lax.axis_index("level")
    strips = lax.axis_size("col") * lax.axis_size("level")
    row_index = lax.axis_index("row")
    flags = jnp.stack(
        [row_index == 0, row_index == lax.axis_size("row") - 1, strip == 0, strip == strips - 1]
    ).astype(jnp.int32)
    tile_rows, tile_cols = friction.shape[1], friction.shape[2]
    out_rows, out_cols = tile_rows // 2, tile_cols // 2

    noise = with_halo(jnp.concatenate([friction, height], axis=0))
    lead = FINE_SHAPE[0] - tile_rows - HALO
    fine_inflow = wrapped_rows(inflow, row_index * tile_rows, FINE_SHAPE[0], lead)
    lead = COARSE_SHAPE[0] - out_rows - 1
    coarse_inflow = wrapped_rows(pair_mean(inflow), row_index * out_rows, COARSE_SHAPE[0], lead)

    out = jax.ShapeDtypeStruct((3, out_rows, out_cols), jnp.float32)
    vmem = pl.BlockSpec(memory_space=pltpu.VMEM)
    mean, corr = pl.pallas_call(
        level_kernel,
        out_shape=(out, out),
        in_specs=[pl.BlockSpec(memory_space=pltpu.SMEM), vmem, vmem, vmem],
        out_specs=(vmem, vmem),
    )(flags, noise, fine_inflow, coarse_inflow)
    return (mean[None], corr[None])


def solution(mesh):
    in_specs = (P("level", "row", "col"), P("level", "row", "col"), P())
    out_specs = (P("level", None, "row", "col"), P("level", None, "row", "col"))
    return jax.shard_map(body, mesh=mesh, in_specs=in_specs, out_specs=out_specs, check_vma=False)
```

```python
import jax
import jax.numpy as jnp
from jax import lax
from jax.experimental import pallas as pl
from jax.experimental.pallas import tpu as pltpu
from jax.sharding import PartitionSpec as P

step_ratio = 0.15
fine_step = 0.15
coarse_step = 0.3
HALO = 2
FINE_SHAPE = (72, 384)
COARSE_SHAPE = (40, 256)


def pair_mean(values):
    paired = values.reshape(-1, 2)
    return (paired[:, 0] + paired[:, 1]) * 0.5


def swap_pairs(count, parity, place=lambda i: i):
    pairs = []
    for i in range(parity, count - 1, 2):
        pairs += [(place(i), place(i + 1)), (place(i + 1), place(i))]
    return pairs


def strip_place(strip):
    levels = lax.axis_size("level")
    return (strip % levels) * lax.axis_size("col") + strip // levels


def swapped(first, last, index, count, axis, place=lambda i: i):
    odd = index % 2 == 1
    got = []
    for parity in range(2):
        sends_last = odd if parity else jnp.logical_not(odd)
        block = jnp.where(sends_last, last, first)
        got.append(lax.ppermute(block, axis, swap_pairs(count, parity, place)))
    before = jnp.where(odd, got[0], got[1])
    after = jnp.where(odd, got[1], got[0])
    return before, after


def with_halo(noise):
    fields, count_rows, count_cols = noise.shape
    strips = lax.axis_size("col") * lax.axis_size("level")
    strip = lax.axis_index("col") * lax.axis_size("level") + lax.axis_index("level")
    rows = lax.axis_size("row")
    north, south = swapped(
        noise[:, :HALO], noise[:, -HALO:], lax.axis_index("row"), rows, "row"
    )
    gap_rows = FINE_SHAPE[0] - count_rows - 2 * HALO
    tall = jnp.concatenate(
        [noise, south, jnp.zeros((fields, gap_rows, count_cols), noise.dtype), north], axis=1
    )
    west, east = swapped(
        tall[:, :, :HALO], tall[:, :, -HALO:], strip, strips, ("level", "col"), strip_place
    )
    gap_cols = FINE_SHAPE[1] - count_cols - 2 * HALO
    return jnp.concatenate(
        [tall, east, jnp.zeros((fields, FINE_SHAPE[0], gap_cols), noise.dtype), west], axis=2
    )


def wrapped_rows(values, start, count, lead):
    padded = jnp.pad(values, lead)
    window = lax.dynamic_slice_in_dim(padded, start, count)
    return (0.5 + jnp.roll(window, -lead)).reshape(count, 1)


def next_of(values, axis):
    return pltpu.roll(values, values.shape[axis] - 1, axis)


def prev_of(values, axis):
    return pltpu.roll(values, 1, axis)


def apply_walls(state, flags, inflow_speed, bottom_row, right_col):
    depth, along_cols, along_rows = state
    shape = depth.shape
    row_at = lax.broadcasted_iota(jnp.int32, shape, 0)
    col_at = lax.broadcasted_iota(jnp.int32, shape, 1)
    top = jnp.logical_and(row_at == shape[0] - 1, flags[0] == 1)
    bottom = jnp.logical_and(row_at == bottom_row, flags[1] == 1)
    left = jnp.logical_and(col_at == shape[1] - 1, flags[2] == 1)
    right = jnp.logical_and(col_at == right_col, flags[3] == 1)

    def rows_fixed(values, sign):
        below = next_of(values, 0)
        above = prev_of(values, 0)
        if sign < 0:
            below = -below
            above = -above
        return jnp.where(top, below, jnp.where(bottom, above, values))

    depth = rows_fixed(depth, 1)
    along_cols = rows_fixed(along_cols, 1)
    along_rows = rows_fixed(along_rows, -1)
    source = next_of(depth, 1)
    entering = (source, source * inflow_speed, jnp.zeros_like(source))
    fixed = []
    for values, inflowing in zip((depth, along_cols, along_rows), entering):
        fixed.append(jnp.where(left, inflowing, jnp.where(right, prev_of(values, 1), values)))
    return tuple(fixed)


def face_flux(state, flux, speed, axis):
    reach = 0.5 * jnp.maximum(next_of(speed, axis), speed)
    return [
        0.5 * (next_of(f, axis) + f) - reach * (next_of(u, axis) - u)
        for f, u in zip(flux, state)
    ]


def advance(state, friction_coef, step):
    depth, along_cols, along_rows = state
    velocity = along_cols / depth
    flux = (along_cols, along_cols * velocity + 0.5 * depth * depth, along_rows * velocity)
    face_x = face_flux(state, flux, jnp.abs(velocity) + jnp.sqrt(depth), 1)
    velocity = along_rows / depth
    flux = (along_rows, along_cols * velocity, along_rows * velocity + 0.5 * depth * depth)
    face_y = face_flux(state, flux, jnp.abs(velocity) + jnp.sqrt(depth), 0)
    moved = [
        u - step_ratio * (fx - prev_of(fx, 1) + (fy - prev_of(fy, 0)))
        for u, fx, fy in zip(state, face_x, face_y)
    ]
    depth = moved[0]
    speed = jnp.sqrt(moved[1] * moved[1] + moved[2] * moved[2]) / depth
    damping = 1.0 / (1.0 + step * friction_coef * speed / depth)
    return (depth, moved[1] * damping, moved[2] * damping)


def pair_matrix(shape, out_axis, last_from):
    out_at = lax.broadcasted_iota(jnp.int32, shape, out_axis)
    in_at = lax.broadcasted_iota(jnp.int32, shape, 1 - out_axis)
    hit = jnp.right_shift(in_at, 1) == out_at
    if last_from is not None:
        last = shape[out_axis] - 1
        hit = jnp.logical_or(hit, jnp.logical_and(out_at == last, in_at >= last_from))
    return hit.astype(jnp.float32)


def matmul(a, b):
    return jnp.dot(a, b, precision=lax.Precision.HIGHEST, preferred_element_type=jnp.float32)


def level_kernel(flags_ref, noise_ref, fine_inflow_ref, coarse_inflow_ref, mean_ref, corr_ref):
    flags = [flags_ref[i] for i in range(4)]
    fine_rows, fine_cols = FINE_SHAPE
    coarse_rows, coarse_cols = COARSE_SHAPE
    out_rows, out_cols = mean_ref.shape[1], mean_ref.shape[2]
    tile_rows, tile_cols = 2 * out_rows, 2 * out_cols

    fine_coef = noise_ref[0]
    noise_height = noise_ref[1]
    depth = 1.0 + 0.1 * noise_height
    state = (depth, 0.5 * depth, jnp.zeros_like(depth))
    fine_inflow = jnp.broadcast_to(fine_inflow_ref[...], FINE_SHAPE)
    for _ in range(2):
        state = apply_walls(state, flags, fine_inflow, tile_rows, tile_cols)
        state = advance(state, fine_coef, fine_step)

    rows_sum = pair_matrix((coarse_rows, fine_rows), 0, fine_rows - 2)
    cols_sum = pair_matrix((fine_cols, coarse_cols), 1, fine_cols - 2)
    coarse_coef = matmul(matmul(rows_sum, fine_coef), cols_sum) * 0.25
    depth = 1.0 + 0.1 * (matmul(matmul(rows_sum, noise_height), cols_sum) * 0.25)
    coarse = (depth, 0.5 * depth, jnp.zeros_like(depth))
    coarse_inflow = jnp.broadcast_to(coarse_inflow_ref[...], COARSE_SHAPE)
    coarse = apply_walls(coarse, flags, coarse_inflow, out_rows, out_cols)
    coarse = advance(coarse, coarse_coef, coarse_step)

    rows_out = pair_matrix((out_rows, tile_rows), 0, None)
    cols_out = pair_matrix((tile_cols, out_cols), 1, None)
    for field in range(3):
        fine_part = state[field][:tile_rows, :tile_cols]
        mean = matmul(matmul(rows_out, fine_part), cols_out) * 0.25
        mean_ref[field] = mean
        corr_ref[field] = mean - coarse[field][:out_rows, :out_cols]


def body(friction, height, inflow):
    strip = lax.axis_index("col") * lax.axis_size("level") + lax.axis_index("level")
    strips = lax.axis_size("col") * lax.axis_size("level")
    row_index = lax.axis_index("row")
    flags = jnp.stack(
        [row_index == 0, row_index == lax.axis_size("row") - 1, strip == 0, strip == strips - 1]
    ).astype(jnp.int32)
    tile_rows, tile_cols = friction.shape[1], friction.shape[2]
    out_rows, out_cols = tile_rows // 2, tile_cols // 2

    noise = with_halo(jnp.concatenate([friction, height], axis=0))
    lead = FINE_SHAPE[0] - tile_rows - HALO
    fine_inflow = wrapped_rows(inflow, row_index * tile_rows, FINE_SHAPE[0], lead)
    lead = COARSE_SHAPE[0] - out_rows - 1
    coarse_inflow = wrapped_rows(pair_mean(inflow), row_index * out_rows, COARSE_SHAPE[0], lead)

    out = jax.ShapeDtypeStruct((3, out_rows, out_cols), jnp.float32)
    vmem = pl.BlockSpec(memory_space=pltpu.VMEM)
    mean, corr = pl.pallas_call(
        level_kernel,
        out_shape=(out, out),
        in_specs=[pl.BlockSpec(memory_space=pltpu.SMEM), vmem, vmem, vmem],
        out_specs=(vmem, vmem),
    )(flags, noise, fine_inflow, coarse_inflow)
    return (mean[None], corr[None])


def solution(mesh):
    in_specs = (P("level", "row", "col"), P("level", "row", "col"), P())
    out_specs = (P("level", None, "row", "col"), P("level", None, "row", "col"))
    return jax.shard_map(body, mesh=mesh, in_specs=in_specs, out_specs=out_specs, check_vma=False)
```

```python
import jax
import jax.numpy as jnp
from jax import lax
from jax.experimental import pallas as pl
from jax.experimental.pallas import tpu as pltpu
from jax.sharding import PartitionSpec as P

step_ratio = 0.15
fine_step = 0.15
coarse_step = 0.3
HALO = 2
FINE_SHAPE = (72, 384)
COARSE_SHAPE = (40, 256)


def pair_mean(values):
    paired = values.reshape(-1, 2)
    return (paired[:, 0] + paired[:, 1]) * 0.5


def swap_pairs(count, parity, place=lambda i: i):
    pairs = []
    for i in range(parity, count - 1, 2):
        pairs += [(place(i), place(i + 1)), (place(i + 1), place(i))]
    return pairs


def strip_place(strip):
    levels = lax.axis_size("level")
    return (strip % levels) * lax.axis_size("col") + strip // levels


def swapped(first, last, index, count, axis, place=lambda i: i):
    odd = index % 2 == 1
    got = []
    for parity in range(2):
        sends_last = odd if parity else jnp.logical_not(odd)
        block = jnp.where(sends_last, last, first)
        got.append(lax.ppermute(block, axis, swap_pairs(count, parity, place)))
    before = jnp.where(odd, got[0], got[1])
    after = jnp.where(odd, got[1], got[0])
    return before, after


def halo_frames(friction, height):
    count_rows, count_cols = friction.shape
    fields = 2
    strips = lax.axis_size("col") * lax.axis_size("level")
    strip = lax.axis_index("col") * lax.axis_size("level") + lax.axis_index("level")
    rows = lax.axis_size("row")

    def both(part):
        return jnp.stack([friction[part], height[part]])

    north, south = swapped(
        both(slice(0, HALO)), both(slice(count_rows - HALO, count_rows)),
        lax.axis_index("row"), rows, "row",
    )
    gap_rows = FINE_SHAPE[0] - count_rows - 2 * HALO
    row_frame = jnp.concatenate(
        [south, jnp.zeros((fields, gap_rows, count_cols), friction.dtype), north], axis=1
    )
    first = (slice(None), slice(0, HALO))
    last = (slice(None), slice(count_cols - HALO, count_cols))
    west, east = swapped(
        jnp.concatenate([both(first), row_frame[:, :, :HALO]], axis=1),
        jnp.concatenate([both(last), row_frame[:, :, -HALO:]], axis=1),
        strip, strips, ("level", "col"), strip_place,
    )
    gap_cols = FINE_SHAPE[1] - count_cols - 2 * HALO
    col_frame = jnp.concatenate(
        [east, jnp.zeros((fields, FINE_SHAPE[0], gap_cols), friction.dtype), west], axis=2
    )
    return row_frame, col_frame


def wrapped_rows(values, start, count, lead):
    padded = jnp.pad(values, lead)
    window = lax.dynamic_slice_in_dim(padded, start, count)
    return (0.5 + jnp.roll(window, -lead)).reshape(count, 1)


def next_of(values, axis):
    return pltpu.roll(values, values.shape[axis] - 1, axis)


def prev_of(values, axis):
    return pltpu.roll(values, 1, axis)


def apply_walls(state, flags, inflow_speed, bottom_row, right_col):
    depth, along_cols, along_rows = state
    shape = depth.shape
    row_at = lax.broadcasted_iota(jnp.int32, shape, 0)
    col_at = lax.broadcasted_iota(jnp.int32, shape, 1)
    top = jnp.logical_and(row_at == shape[0] - 1, flags[0] == 1)
    bottom = jnp.logical_and(row_at == bottom_row, flags[1] == 1)
    left = jnp.logical_and(col_at == shape[1] - 1, flags[2] == 1)
    right = jnp.logical_and(col_at == right_col, flags[3] == 1)

    def rows_fixed(values, sign):
        below = next_of(values, 0)
        above = prev_of(values, 0)
        if sign < 0:
            below = -below
            above = -above
        return jnp.where(top, below, jnp.where(bottom, above, values))

    depth = rows_fixed(depth, 1)
    along_cols = rows_fixed(along_cols, 1)
    along_rows = rows_fixed(along_rows, -1)
    source = next_of(depth, 1)
    entering = (source, source * inflow_speed, jnp.zeros_like(source))
    fixed = []
    for values, inflowing in zip((depth, along_cols, along_rows), entering):
        fixed.append(jnp.where(left, inflowing, jnp.where(right, prev_of(values, 1), values)))
    return tuple(fixed)


def face_flux(state, flux, speed, axis):
    reach = 0.5 * jnp.maximum(next_of(speed, axis), speed)
    return [
        0.5 * (next_of(f, axis) + f) - reach * (next_of(u, axis) - u)
        for f, u in zip(flux, state)
    ]


def advance(state, friction_coef, step):
    depth, along_cols, along_rows = state
    velocity = along_cols / depth
    flux = (along_cols, along_cols * velocity + 0.5 * depth * depth, along_rows * velocity)
    face_x = face_flux(state, flux, jnp.abs(velocity) + jnp.sqrt(depth), 1)
    velocity = along_rows / depth
    flux = (along_rows, along_cols * velocity, along_rows * velocity + 0.5 * depth * depth)
    face_y = face_flux(state, flux, jnp.abs(velocity) + jnp.sqrt(depth), 0)
    moved = [
        u - step_ratio * (fx - prev_of(fx, 1) + (fy - prev_of(fy, 0)))
        for u, fx, fy in zip(state, face_x, face_y)
    ]
    depth = moved[0]
    speed = jnp.sqrt(moved[1] * moved[1] + moved[2] * moved[2]) / depth
    damping = 1.0 / (1.0 + step * friction_coef * speed / depth)
    return (depth, moved[1] * damping, moved[2] * damping)


def pair_matrix(shape, out_axis, last_from):
    out_at = lax.broadcasted_iota(jnp.int32, shape, out_axis)
    in_at = lax.broadcasted_iota(jnp.int32, shape, 1 - out_axis)
    hit = jnp.right_shift(in_at, 1) == out_at
    if last_from is not None:
        last = shape[out_axis] - 1
        hit = jnp.logical_or(hit, jnp.logical_and(out_at == last, in_at >= last_from))
    return hit.astype(jnp.float32)


def matmul(a, b):
    return jnp.dot(a, b, precision=lax.Precision.HIGHEST, preferred_element_type=jnp.float32)


def level_kernel(
    flags_ref, friction_ref, height_ref, row_frame_ref, col_frame_ref, fine_inflow_ref,
    coarse_inflow_ref, mean_ref, corr_ref,
):
    flags = [flags_ref[i] for i in range(4)]

    def framed(center_ref, field):
        tall = jnp.concatenate([center_ref[0], row_frame_ref[field]], axis=0)
        return jnp.concatenate([tall, col_frame_ref[field]], axis=1)

    fine_rows, fine_cols = FINE_SHAPE
    coarse_rows, coarse_cols = COARSE_SHAPE
    out_rows, out_cols = mean_ref.shape[1], mean_ref.shape[2]
    tile_rows, tile_cols = 2 * out_rows, 2 * out_cols

    fine_coef = framed(friction_ref, 0)
    noise_height = framed(height_ref, 1)
    depth = 1.0 + 0.1 * noise_height
    state = (depth, 0.5 * depth, jnp.zeros_like(depth))
    fine_inflow = jnp.broadcast_to(fine_inflow_ref[...], FINE_SHAPE)
    for _ in range(2):
        state = apply_walls(state, flags, fine_inflow, tile_rows, tile_cols)
        state = advance(state, fine_coef, fine_step)

    rows_sum = pair_matrix((coarse_rows, fine_rows), 0, fine_rows - 2)
    cols_sum = pair_matrix((fine_cols, coarse_cols), 1, fine_cols - 2)
    coarse_coef = matmul(matmul(rows_sum, fine_coef), cols_sum) * 0.25
    depth = 1.0 + 0.1 * (matmul(matmul(rows_sum, noise_height), cols_sum) * 0.25)
    coarse = (depth, 0.5 * depth, jnp.zeros_like(depth))
    coarse_inflow = jnp.broadcast_to(coarse_inflow_ref[...], COARSE_SHAPE)
    coarse = apply_walls(coarse, flags, coarse_inflow, out_rows, out_cols)
    coarse = advance(coarse, coarse_coef, coarse_step)

    rows_out = pair_matrix((out_rows, tile_rows), 0, None)
    cols_out = pair_matrix((tile_cols, out_cols), 1, None)
    for field in range(3):
        fine_part = state[field][:tile_rows, :tile_cols]
        mean = matmul(matmul(rows_out, fine_part), cols_out) * 0.25
        mean_ref[field] = mean
        corr_ref[field] = mean - coarse[field][:out_rows, :out_cols]


def body(friction, height, inflow):
    strip = lax.axis_index("col") * lax.axis_size("level") + lax.axis_index("level")
    strips = lax.axis_size("col") * lax.axis_size("level")
    row_index = lax.axis_index("row")
    flags = jnp.stack(
        [row_index == 0, row_index == lax.axis_size("row") - 1, strip == 0, strip == strips - 1]
    ).astype(jnp.int32)
    tile_rows, tile_cols = friction.shape[1], friction.shape[2]
    out_rows, out_cols = tile_rows // 2, tile_cols // 2

    row_frame, col_frame = halo_frames(friction[0], height[0])
    lead = FINE_SHAPE[0] - tile_rows - HALO
    fine_inflow = wrapped_rows(inflow, row_index * tile_rows, FINE_SHAPE[0], lead)
    lead = COARSE_SHAPE[0] - out_rows - 1
    coarse_inflow = wrapped_rows(pair_mean(inflow), row_index * out_rows, COARSE_SHAPE[0], lead)

    out = jax.ShapeDtypeStruct((3, out_rows, out_cols), jnp.float32)
    vmem = pl.BlockSpec(memory_space=pltpu.VMEM)
    mean, corr = pl.pallas_call(
        level_kernel,
        out_shape=(out, out),
        in_specs=[pl.BlockSpec(memory_space=pltpu.SMEM)] + [vmem] * 6,
        out_specs=(vmem, vmem),
    )(flags, friction, height, row_frame, col_frame, fine_inflow, coarse_inflow)
    return (mean[None], corr[None])


def solution(mesh):
    in_specs = (P("level", "row", "col"), P("level", "row", "col"), P())
    out_specs = (P("level", None, "row", "col"), P("level", None, "row", "col"))
    return jax.shard_map(body, mesh=mesh, in_specs=in_specs, out_specs=out_specs, check_vma=False)
```

```python
import jax
import jax.numpy as jnp
from jax import lax
from jax.experimental import pallas as pl
from jax.experimental.pallas import tpu as pltpu
from jax.sharding import PartitionSpec as P

step_ratio = 0.15
fine_step = 0.15
coarse_step = 0.3
HALO = 2
FINE_SHAPE = (72, 384)
COARSE_SHAPE = (40, 256)


def pair_mean(values):
    paired = values.reshape(-1, 2)
    return (paired[:, 0] + paired[:, 1]) * 0.5


def swap_pairs(count, parity, place=lambda i: i):
    pairs = []
    for i in range(parity, count - 1, 2):
        pairs += [(place(i), place(i + 1)), (place(i + 1), place(i))]
    return pairs


def strip_place(strip):
    levels = lax.axis_size("level")
    return (strip % levels) * lax.axis_size("col") + strip // levels


def swapped(first, last, index, count, axis, place=lambda i: i):
    odd = index % 2 == 1
    got = []
    for parity in range(2):
        sends_last = odd if parity else jnp.logical_not(odd)
        block = jnp.where(sends_last, last, first)
        got.append(lax.ppermute(block, axis, swap_pairs(count, parity, place)))
    return got


def by_parity(got, odd):
    before = jnp.where(odd, got[0], got[1])
    after = jnp.where(odd, got[1], got[0])
    return before, after


def halo_tiles(friction, height):
    count_rows, count_cols = friction.shape
    fields = 2
    strips = lax.axis_size("col") * lax.axis_size("level")
    strip = lax.axis_index("col") * lax.axis_size("level") + lax.axis_index("level")
    row_index = lax.axis_index("row")
    tile_rows, tile_cols = 8, 128

    def both(rows):
        return jnp.stack([friction[rows], height[rows]])

    row_got = swapped(
        both(slice(0, tile_rows)), both(slice(count_rows - tile_rows, count_rows)),
        row_index, lax.axis_size("row"), "row",
    )
    north, south = by_parity(row_got, row_index % 2 == 1)
    sub_at = lax.broadcasted_iota(jnp.int32, (fields, tile_rows, count_cols), 1)
    row_frame = jnp.where(sub_at < tile_rows // 2, south, north)
    tall = jnp.concatenate([jnp.stack([friction, height]), row_frame], axis=1)
    col_got = swapped(
        tall[:, :, :tile_cols], tall[:, :, count_cols - tile_cols:],
        strip, strips, ("level", "col"), strip_place,
    )
    return row_got, col_got


def wrapped_rows(values, start, count, lead):
    padded = jnp.pad(values, lead)
    window = lax.dynamic_slice_in_dim(padded, start, count)
    return (0.5 + jnp.roll(window, -lead)).reshape(count, 1)


def next_of(values, axis):
    return pltpu.roll(values, values.shape[axis] - 1, axis)


def prev_of(values, axis):
    return pltpu.roll(values, 1, axis)


def apply_walls(state, flags, inflow_speed, bottom_row, right_col):
    depth, along_cols, along_rows = state
    shape = depth.shape
    row_at = lax.broadcasted_iota(jnp.int32, shape, 0)
    col_at = lax.broadcasted_iota(jnp.int32, shape, 1)
    top = jnp.logical_and(row_at == shape[0] - 1, flags[0] == 1)
    bottom = jnp.logical_and(row_at == bottom_row, flags[1] == 1)
    left = jnp.logical_and(col_at == shape[1] - 1, flags[2] == 1)
    right = jnp.logical_and(col_at == right_col, flags[3] == 1)

    def rows_fixed(values, sign):
        below = next_of(values, 0)
        above = prev_of(values, 0)
        if sign < 0:
            below = -below
            above = -above
        return jnp.where(top, below, jnp.where(bottom, above, values))

    depth = rows_fixed(depth, 1)
    along_cols = rows_fixed(along_cols, 1)
    along_rows = rows_fixed(along_rows, -1)
    source = next_of(depth, 1)
    entering = (source, source * inflow_speed, jnp.zeros_like(source))
    fixed = []
    for values, inflowing in zip((depth, along_cols, along_rows), entering):
        fixed.append(jnp.where(left, inflowing, jnp.where(right, prev_of(values, 1), values)))
    return tuple(fixed)


def face_flux(state, flux, speed, axis):
    reach = 0.5 * jnp.maximum(next_of(speed, axis), speed)
    return [
        0.5 * (next_of(f, axis) + f) - reach * (next_of(u, axis) - u)
        for f, u in zip(flux, state)
    ]


def advance(state, friction_coef, step):
    depth, along_cols, along_rows = state
    velocity = along_cols / depth
    flux = (along_cols, along_cols * velocity + 0.5 * depth * depth, along_rows * velocity)
    face_x = face_flux(state, flux, jnp.abs(velocity) + jnp.sqrt(depth), 1)
    velocity = along_rows / depth
    flux = (along_rows, along_cols * velocity, along_rows * velocity + 0.5 * depth * depth)
    face_y = face_flux(state, flux, jnp.abs(velocity) + jnp.sqrt(depth), 0)
    moved = [
        u - step_ratio * (fx - prev_of(fx, 1) + (fy - prev_of(fy, 0)))
        for u, fx, fy in zip(state, face_x, face_y)
    ]
    depth = moved[0]
    speed = jnp.sqrt(moved[1] * moved[1] + moved[2] * moved[2]) / depth
    damping = 1.0 / (1.0 + step * friction_coef * speed / depth)
    return (depth, moved[1] * damping, moved[2] * damping)


def pair_matrix(shape, out_axis, last_from):
    out_at = lax.broadcasted_iota(jnp.int32, shape, out_axis)
    in_at = lax.broadcasted_iota(jnp.int32, shape, 1 - out_axis)
    hit = jnp.right_shift(in_at, 1) == out_at
    if last_from is not None:
        last = shape[out_axis] - 1
        hit = jnp.logical_or(hit, jnp.logical_and(out_at == last, in_at >= last_from))
    return hit.astype(jnp.float32)


def matmul(a, b):
    return jnp.dot(a, b, precision=lax.Precision.HIGHEST, preferred_element_type=jnp.float32)


def level_kernel(
    flags_ref, friction_ref, height_ref, row_first_ref, row_second_ref, col_first_ref,
    col_second_ref, fine_inflow_ref, coarse_inflow_ref, mean_ref, corr_ref,
):
    flags = [flags_ref[i] for i in range(4)]
    odd_row = flags_ref[4] == 1
    odd_strip = flags_ref[5] == 1

    def framed(center_ref, field):
        north, south = by_parity((row_first_ref[field], row_second_ref[field]), odd_row)
        sub_at = lax.broadcasted_iota(jnp.int32, north.shape, 0)
        tall = jnp.concatenate(
            [center_ref[0], jnp.where(sub_at < north.shape[0] // 2, south, north)], axis=0
        )
        west, east = by_parity((col_first_ref[field], col_second_ref[field]), odd_strip)
        lane_at = lax.broadcasted_iota(jnp.int32, east.shape, 1)
        return jnp.concatenate([tall, jnp.where(lane_at < east.shape[1] // 2, east, west)], axis=1)

    fine_rows, fine_cols = FINE_SHAPE
    coarse_rows, coarse_cols = COARSE_SHAPE
    out_rows, out_cols = mean_ref.shape[1], mean_ref.shape[2]
    tile_rows, tile_cols = 2 * out_rows, 2 * out_cols

    fine_coef = framed(friction_ref, 0)
    noise_height = framed(height_ref, 1)
    depth = 1.0 + 0.1 * noise_height
    state = (depth, 0.5 * depth, jnp.zeros_like(depth))
    fine_inflow = jnp.broadcast_to(fine_inflow_ref[...], FINE_SHAPE)
    for _ in range(2):
        state = apply_walls(state, flags, fine_inflow, tile_rows, tile_cols)
        state = advance(state, fine_coef, fine_step)

    rows_sum = pair_matrix((coarse_rows, fine_rows), 0, fine_rows - 2)
    cols_sum = pair_matrix((fine_cols, coarse_cols), 1, fine_cols - 2)
    coarse_coef = matmul(matmul(rows_sum, fine_coef), cols_sum) * 0.25
    depth = 1.0 + 0.1 * (matmul(matmul(rows_sum, noise_height), cols_sum) * 0.25)
    coarse = (depth, 0.5 * depth, jnp.zeros_like(depth))
    coarse_inflow = jnp.broadcast_to(coarse_inflow_ref[...], COARSE_SHAPE)
    coarse = apply_walls(coarse, flags, coarse_inflow, out_rows, out_cols)
    coarse = advance(coarse, coarse_coef, coarse_step)

    rows_out = pair_matrix((out_rows, tile_rows), 0, None)
    cols_out = pair_matrix((tile_cols, out_cols), 1, None)
    for field in range(3):
        fine_part = state[field][:tile_rows, :tile_cols]
        mean = matmul(matmul(rows_out, fine_part), cols_out) * 0.25
        mean_ref[field] = mean
        corr_ref[field] = mean - coarse[field][:out_rows, :out_cols]


def body(friction, height, inflow):
    strip = lax.axis_index("col") * lax.axis_size("level") + lax.axis_index("level")
    strips = lax.axis_size("col") * lax.axis_size("level")
    row_index = lax.axis_index("row")
    flags = jnp.stack(
        [row_index == 0, row_index == lax.axis_size("row") - 1, strip == 0, strip == strips - 1,
         row_index % 2 == 1, strip % 2 == 1]
    ).astype(jnp.int32)
    tile_rows, tile_cols = friction.shape[1], friction.shape[2]
    out_rows, out_cols = tile_rows // 2, tile_cols // 2

    row_got, col_got = halo_tiles(friction[0], height[0])
    lead = FINE_SHAPE[0] - tile_rows - HALO
    fine_inflow = wrapped_rows(inflow, row_index * tile_rows, FINE_SHAPE[0], lead)
    lead = COARSE_SHAPE[0] - out_rows - 1
    coarse_inflow = wrapped_rows(pair_mean(inflow), row_index * out_rows, COARSE_SHAPE[0], lead)

    out = jax.ShapeDtypeStruct((3, out_rows, out_cols), jnp.float32)
    vmem = pl.BlockSpec(memory_space=pltpu.VMEM)
    mean, corr = pl.pallas_call(
        level_kernel,
        out_shape=(out, out),
        in_specs=[pl.BlockSpec(memory_space=pltpu.SMEM)] + [vmem] * 8,
        out_specs=(vmem, vmem),
    )(flags, friction, height, *row_got, *col_got, fine_inflow, coarse_inflow)
    return (mean[None], corr[None])


def solution(mesh):
    in_specs = (P("level", "row", "col"), P("level", "row", "col"), P())
    out_specs = (P("level", None, "row", "col"), P("level", None, "row", "col"))
    return jax.shard_map(body, mesh=mesh, in_specs=in_specs, out_specs=out_specs, check_vma=False)
```

```python
import jax
import jax.numpy as jnp
from jax import lax
from jax.experimental import pallas as pl
from jax.experimental.pallas import tpu as pltpu
from jax.sharding import PartitionSpec as P

step_ratio = 0.15
fine_step = 0.15
coarse_step = 0.3
HALO = 2
FINE_SHAPE = (72, 384)
COARSE_SHAPE = (40, 256)


def pair_mean(values):
    paired = values.reshape(-1, 2)
    return (paired[:, 0] + paired[:, 1]) * 0.5


def swap_pairs(count, parity, place=lambda i: i):
    pairs = []
    for i in range(parity, count - 1, 2):
        pairs += [(place(i), place(i + 1)), (place(i + 1), place(i))]
    return pairs


def strip_place(strip):
    levels = lax.axis_size("level")
    return (strip % levels) * lax.axis_size("col") + strip // levels


def swapped(first, last, index, count, axis, place=lambda i: i):
    odd = index % 2 == 1
    got = []
    for parity in range(2):
        sends_last = odd if parity else jnp.logical_not(odd)
        block = jnp.where(sends_last, last, first)
        got.append(lax.ppermute(block, axis, swap_pairs(count, parity, place)))
    before = jnp.where(odd, got[0], got[1])
    after = jnp.where(odd, got[1], got[0])
    return before, after


def with_halo(noise):
    fields, count_rows, count_cols = noise.shape
    strips = lax.axis_size("col") * lax.axis_size("level")
    strip = lax.axis_index("col") * lax.axis_size("level") + lax.axis_index("level")
    rows = lax.axis_size("row")
    north, south = swapped(
        noise[:, :HALO], noise[:, -HALO:], lax.axis_index("row"), rows, "row"
    )
    gap_rows = FINE_SHAPE[0] - count_rows - 2 * HALO
    tall = jnp.concatenate(
        [noise, south, jnp.zeros((fields, gap_rows, count_cols), noise.dtype), north], axis=1
    )
    west, east = swapped(
        tall[:, :, :HALO], tall[:, :, -HALO:], strip, strips, ("level", "col"), strip_place
    )
    gap_cols = FINE_SHAPE[1] - count_cols - 2 * HALO
    return jnp.concatenate(
        [tall, east, jnp.zeros((fields, FINE_SHAPE[0], gap_cols), noise.dtype), west], axis=2
    )


def wrapped_rows(values, start, count, lead):
    padded = jnp.pad(values, lead)
    window = lax.dynamic_slice_in_dim(padded, start, count)
    return (0.5 + jnp.roll(window, -lead)).reshape(count, 1)


def next_of(values, axis):
    return pltpu.roll(values, values.shape[axis] - 1, axis)


def prev_of(values, axis):
    return pltpu.roll(values, 1, axis)


def apply_walls(state, flags, inflow_speed, bottom_row, right_col):
    depth, along_cols, along_rows = state
    shape = depth.shape
    row_at = lax.broadcasted_iota(jnp.int32, shape, 0)
    col_at = lax.broadcasted_iota(jnp.int32, shape, 1)
    top = jnp.logical_and(row_at == shape[0] - 1, flags[0] == 1)
    bottom = jnp.logical_and(row_at == bottom_row, flags[1] == 1)
    left = jnp.logical_and(col_at == shape[1] - 1, flags[2] == 1)
    right = jnp.logical_and(col_at == right_col, flags[3] == 1)

    def rows_fixed(values, sign):
        below = next_of(values, 0)
        above = prev_of(values, 0)
        if sign < 0:
            below = -below
            above = -above
        return jnp.where(top, below, jnp.where(bottom, above, values))

    depth = rows_fixed(depth, 1)
    along_cols = rows_fixed(along_cols, 1)
    along_rows = rows_fixed(along_rows, -1)
    source = next_of(depth, 1)
    entering = (source, source * inflow_speed, jnp.zeros_like(source))
    fixed = []
    for values, inflowing in zip((depth, along_cols, along_rows), entering):
        fixed.append(jnp.where(left, inflowing, jnp.where(right, prev_of(values, 1), values)))
    return tuple(fixed)


def face_flux(state, flux, speed, axis):
    reach = 0.5 * jnp.maximum(next_of(speed, axis), speed)
    return [
        0.5 * (next_of(f, axis) + f) - reach * (next_of(u, axis) - u)
        for f, u in zip(flux, state)
    ]


def advance(state, friction_coef, step):
    depth, along_cols, along_rows = state
    velocity = along_cols / depth
    flux = (along_cols, along_cols * velocity + 0.5 * depth * depth, along_rows * velocity)
    face_x = face_flux(state, flux, jnp.abs(velocity) + jnp.sqrt(depth), 1)
    velocity = along_rows / depth
    flux = (along_rows, along_cols * velocity, along_rows * velocity + 0.5 * depth * depth)
    face_y = face_flux(state, flux, jnp.abs(velocity) + jnp.sqrt(depth), 0)
    moved = [
        u - step_ratio * (fx - prev_of(fx, 1) + (fy - prev_of(fy, 0)))
        for u, fx, fy in zip(state, face_x, face_y)
    ]
    depth = moved[0]
    speed = jnp.sqrt(moved[1] * moved[1] + moved[2] * moved[2]) / depth
    damping = 1.0 / (1.0 + step * friction_coef * speed / depth)
    return (depth, moved[1] * damping, moved[2] * damping)


def walls_at_rest(state, flags, inflow_speed, bottom_row, right_col):
    depth, along_cols, _ = state
    depth, along_cols, _ = apply_walls(
        (depth, along_cols, depth), flags, inflow_speed, bottom_row, right_col
    )
    return (depth, along_cols, jnp.zeros_like(depth))


def advance_at_rest(state, friction_coef, step):
    depth, along_cols, _ = state
    velocity = along_cols / depth
    root = jnp.sqrt(depth)
    flux = (along_cols, along_cols * velocity + 0.5 * depth * depth)
    face_x = face_flux((depth, along_cols), flux, jnp.abs(velocity) + root, 1)
    reach = 0.5 * jnp.maximum(next_of(root, 0), root)
    face_y = [0.0 - reach * (next_of(u, 0) - u) for u in (depth, along_cols)]
    pressure = 0.5 * depth * depth
    pressure_face = 0.5 * (next_of(pressure, 0) + pressure)
    moved = [
        u - step_ratio * (fx - prev_of(fx, 1) + (fy - prev_of(fy, 0)))
        for u, fx, fy in zip((depth, along_cols), face_x, face_y)
    ]
    moved.append(0.0 - step_ratio * (pressure_face - prev_of(pressure_face, 0)))
    depth = moved[0]
    speed = jnp.sqrt(moved[1] * moved[1] + moved[2] * moved[2]) / depth
    damping = 1.0 / (1.0 + step * friction_coef * speed / depth)
    return (depth, moved[1] * damping, moved[2] * damping)


def pair_matrix(shape, out_axis, last_from):
    out_at = lax.broadcasted_iota(jnp.int32, shape, out_axis)
    in_at = lax.broadcasted_iota(jnp.int32, shape, 1 - out_axis)
    hit = jnp.right_shift(in_at, 1) == out_at
    if last_from is not None:
        last = shape[out_axis] - 1
        hit = jnp.logical_or(hit, jnp.logical_and(out_at == last, in_at >= last_from))
    return hit.astype(jnp.float32)


def matmul(a, b):
    return jnp.dot(a, b, precision=lax.Precision.HIGHEST, preferred_element_type=jnp.float32)


def level_kernel(flags_ref, noise_ref, fine_inflow_ref, coarse_inflow_ref, mean_ref, corr_ref):
    flags = [flags_ref[i] for i in range(4)]
    fine_rows, fine_cols = FINE_SHAPE
    coarse_rows, coarse_cols = COARSE_SHAPE
    out_rows, out_cols = mean_ref.shape[1], mean_ref.shape[2]
    tile_rows, tile_cols = 2 * out_rows, 2 * out_cols

    fine_coef = noise_ref[0]
    noise_height = noise_ref[1]
    depth = 1.0 + 0.1 * noise_height
    state = (depth, 0.5 * depth, jnp.zeros_like(depth))
    fine_inflow = jnp.broadcast_to(fine_inflow_ref[...], FINE_SHAPE)
    state = walls_at_rest(state, flags, fine_inflow, tile_rows, tile_cols)
    state = advance_at_rest(state, fine_coef, fine_step)
    state = apply_walls(state, flags, fine_inflow, tile_rows, tile_cols)
    state = advance(state, fine_coef, fine_step)

    rows_sum = pair_matrix((coarse_rows, fine_rows), 0, fine_rows - 2)
    cols_sum = pair_matrix((fine_cols, coarse_cols), 1, fine_cols - 2)
    coarse_coef = matmul(matmul(rows_sum, fine_coef), cols_sum) * 0.25
    depth = 1.0 + 0.1 * (matmul(matmul(rows_sum, noise_height), cols_sum) * 0.25)
    coarse = (depth, 0.5 * depth, jnp.zeros_like(depth))
    coarse_inflow = jnp.broadcast_to(coarse_inflow_ref[...], COARSE_SHAPE)
    coarse = walls_at_rest(coarse, flags, coarse_inflow, out_rows, out_cols)
    coarse = advance_at_rest(coarse, coarse_coef, coarse_step)

    rows_out = pair_matrix((out_rows, tile_rows), 0, None)
    cols_out = pair_matrix((tile_cols, out_cols), 1, None)
    for field in range(3):
        fine_part = state[field][:tile_rows, :tile_cols]
        mean = matmul(matmul(rows_out, fine_part), cols_out) * 0.25
        mean_ref[field] = mean
        corr_ref[field] = mean - coarse[field][:out_rows, :out_cols]


def body(friction, height, inflow):
    strip = lax.axis_index("col") * lax.axis_size("level") + lax.axis_index("level")
    strips = lax.axis_size("col") * lax.axis_size("level")
    row_index = lax.axis_index("row")
    flags = jnp.stack(
        [row_index == 0, row_index == lax.axis_size("row") - 1, strip == 0, strip == strips - 1]
    ).astype(jnp.int32)
    tile_rows, tile_cols = friction.shape[1], friction.shape[2]
    out_rows, out_cols = tile_rows // 2, tile_cols // 2

    noise = with_halo(jnp.concatenate([friction, height], axis=0))
    lead = FINE_SHAPE[0] - tile_rows - HALO
    fine_inflow = wrapped_rows(inflow, row_index * tile_rows, FINE_SHAPE[0], lead)
    lead = COARSE_SHAPE[0] - out_rows - 1
    coarse_inflow = wrapped_rows(pair_mean(inflow), row_index * out_rows, COARSE_SHAPE[0], lead)

    out = jax.ShapeDtypeStruct((3, out_rows, out_cols), jnp.float32)
    vmem = pl.BlockSpec(memory_space=pltpu.VMEM)
    mean, corr = pl.pallas_call(
        level_kernel,
        out_shape=(out, out),
        in_specs=[pl.BlockSpec(memory_space=pltpu.SMEM), vmem, vmem, vmem],
        out_specs=(vmem, vmem),
    )(flags, noise, fine_inflow, coarse_inflow)
    return (mean[None], corr[None])


def solution(mesh):
    in_specs = (P("level", "row", "col"), P("level", "row", "col"), P())
    out_specs = (P("level", None, "row", "col"), P("level", None, "row", "col"))
    return jax.shard_map(body, mesh=mesh, in_specs=in_specs, out_specs=out_specs, check_vma=False)
```

```python
import jax
import jax.numpy as jnp
from jax import lax
from jax.experimental import pallas as pl
from jax.experimental.pallas import tpu as pltpu
from jax.sharding import PartitionSpec as P

step_ratio = 0.15
fine_step = 0.15
coarse_step = 0.3
HALO = 2
FINE_SHAPE = (72, 384)
COARSE_SHAPE = (40, 256)


def pair_mean(values):
    paired = values.reshape(-1, 2)
    return (paired[:, 0] + paired[:, 1]) * 0.5


def swap_pairs(count, parity, place=lambda i: i):
    pairs = []
    for i in range(parity, count - 1, 2):
        pairs += [(place(i), place(i + 1)), (place(i + 1), place(i))]
    return pairs


def strip_place(strip):
    levels = lax.axis_size("level")
    return (strip % levels) * lax.axis_size("col") + strip // levels


def swapped(first, last, index, count, axis, place=lambda i: i):
    odd = index % 2 == 1
    got = []
    for parity in range(2):
        sends_last = odd if parity else jnp.logical_not(odd)
        block = jnp.where(sends_last, last, first)
        got.append(lax.ppermute(block, axis, swap_pairs(count, parity, place)))
    before = jnp.where(odd, got[0], got[1])
    after = jnp.where(odd, got[1], got[0])
    return before, after


def with_halo(noise):
    fields, count_rows, count_cols = noise.shape
    strips = lax.axis_size("col") * lax.axis_size("level")
    strip = lax.axis_index("col") * lax.axis_size("level") + lax.axis_index("level")
    rows = lax.axis_size("row")
    north, south = swapped(
        noise[:, :HALO], noise[:, -HALO:], lax.axis_index("row"), rows, "row"
    )
    gap_rows = FINE_SHAPE[0] - count_rows - 2 * HALO
    tall = jnp.concatenate(
        [noise, south, jnp.zeros((fields, gap_rows, count_cols), noise.dtype), north], axis=1
    )
    west, east = swapped(
        tall[:, :, :HALO], tall[:, :, -HALO:], strip, strips, ("level", "col"), strip_place
    )
    gap_cols = FINE_SHAPE[1] - count_cols - 2 * HALO
    return jnp.concatenate(
        [tall, east, jnp.zeros((fields, FINE_SHAPE[0], gap_cols), noise.dtype), west], axis=2
    )


def wrapped_rows(values, start, count, lead):
    padded = jnp.pad(values, lead)
    window = lax.dynamic_slice_in_dim(padded, start, count)
    return (0.5 + jnp.roll(window, -lead)).reshape(count, 1)


def next_of(values, axis):
    return pltpu.roll(values, values.shape[axis] - 1, axis)


def prev_of(values, axis):
    return pltpu.roll(values, 1, axis)


def apply_walls(state, flags, inflow_speed, bottom_row, right_col):
    depth, along_cols, along_rows = state
    shape = depth.shape
    row_at = lax.broadcasted_iota(jnp.int32, shape, 0)
    col_at = lax.broadcasted_iota(jnp.int32, shape, 1)
    top = jnp.logical_and(row_at == shape[0] - 1, flags[0] == 1)
    bottom = jnp.logical_and(row_at == bottom_row, flags[1] == 1)
    left = jnp.logical_and(col_at == shape[1] - 1, flags[2] == 1)
    right = jnp.logical_and(col_at == right_col, flags[3] == 1)

    def rows_fixed(values, sign):
        below = next_of(values, 0)
        above = prev_of(values, 0)
        if sign < 0:
            below = -below
            above = -above
        return jnp.where(top, below, jnp.where(bottom, above, values))

    depth = rows_fixed(depth, 1)
    along_cols = rows_fixed(along_cols, 1)
    along_rows = rows_fixed(along_rows, -1)
    source = next_of(depth, 1)
    entering = (source, source * inflow_speed, jnp.zeros_like(source))
    fixed = []
    for values, inflowing in zip((depth, along_cols, along_rows), entering):
        fixed.append(jnp.where(left, inflowing, jnp.where(right, prev_of(values, 1), values)))
    return tuple(fixed)


def face_flux(state, flux, speed, axis):
    reach = 0.5 * jnp.maximum(next_of(speed, axis), speed)
    return [
        0.5 * (next_of(f, axis) + f) - reach * (next_of(u, axis) - u)
        for f, u in zip(flux, state)
    ]


def advance(state, friction_coef, step):
    depth, along_cols, along_rows = state
    velocity = along_cols / depth
    flux = (along_cols, along_cols * velocity + 0.5 * depth * depth, along_rows * velocity)
    face_x = face_flux(state, flux, jnp.abs(velocity) + jnp.sqrt(depth), 1)
    velocity = along_rows / depth
    flux = (along_rows, along_cols * velocity, along_rows * velocity + 0.5 * depth * depth)
    face_y = face_flux(state, flux, jnp.abs(velocity) + jnp.sqrt(depth), 0)
    moved = [
        u - step_ratio * (fx - prev_of(fx, 1) + (fy - prev_of(fy, 0)))
        for u, fx, fy in zip(state, face_x, face_y)
    ]
    depth = moved[0]
    speed = jnp.sqrt(moved[1] * moved[1] + moved[2] * moved[2]) / depth
    damping = 1.0 / (1.0 + step * friction_coef * speed / depth)
    return (depth, moved[1] * damping, moved[2] * damping)


def walls_at_rest(state, flags, inflow_speed, bottom_row, right_col):
    depth, along_cols, _ = state
    depth, along_cols, _ = apply_walls(
        (depth, along_cols, depth), flags, inflow_speed, bottom_row, right_col
    )
    return (depth, along_cols, jnp.zeros_like(depth))


def advance_at_rest(state, friction_coef, step):
    depth, along_cols, _ = state
    velocity = along_cols / depth
    root = jnp.sqrt(depth)
    flux = (along_cols, along_cols * velocity + 0.5 * depth * depth)
    face_x = face_flux((depth, along_cols), flux, jnp.abs(velocity) + root, 1)
    reach = 0.5 * jnp.maximum(next_of(root, 0), root)
    face_y = [0.0 - reach * (next_of(u, 0) - u) for u in (depth, along_cols)]
    pressure = 0.5 * depth * depth
    pressure_face = 0.5 * (next_of(pressure, 0) + pressure)
    moved = [
        u - step_ratio * (fx - prev_of(fx, 1) + (fy - prev_of(fy, 0)))
        for u, fx, fy in zip((depth, along_cols), face_x, face_y)
    ]
    moved.append(0.0 - step_ratio * (pressure_face - prev_of(pressure_face, 0)))
    depth = moved[0]
    speed = jnp.sqrt(moved[1] * moved[1] + moved[2] * moved[2]) / depth
    damping = 1.0 / (1.0 + step * friction_coef * speed / depth)
    return (depth, moved[1] * damping, moved[2] * damping)


def pair_matrix(shape, out_axis, last_from):
    out_at = lax.broadcasted_iota(jnp.int32, shape, out_axis)
    in_at = lax.broadcasted_iota(jnp.int32, shape, 1 - out_axis)
    hit = jnp.right_shift(in_at, 1) == out_at
    if last_from is not None:
        last = shape[out_axis] - 1
        hit = jnp.logical_or(hit, jnp.logical_and(out_at == last, in_at >= last_from))
    return hit.astype(jnp.float32)


def matmul(a, b):
    return jnp.dot(a, b, precision=lax.Precision.HIGHEST, preferred_element_type=jnp.float32)


def level_kernel(flags_ref, noise_ref, fine_inflow_ref, coarse_inflow_ref, mean_ref, corr_ref):
    flags = [flags_ref[i] for i in range(4)]
    fine_rows, fine_cols = FINE_SHAPE
    coarse_rows, coarse_cols = COARSE_SHAPE
    out_rows, out_cols = mean_ref.shape[1], mean_ref.shape[2]
    tile_rows, tile_cols = 2 * out_rows, 2 * out_cols

    fine_coef = noise_ref[0]
    noise_height = noise_ref[1]
    depth = 1.0 + 0.1 * noise_height
    state = (depth, 0.5 * depth, jnp.zeros_like(depth))
    fine_inflow = jnp.broadcast_to(fine_inflow_ref[...], FINE_SHAPE)
    state = walls_at_rest(state, flags, fine_inflow, tile_rows, tile_cols)
    state = advance_at_rest(state, fine_coef, fine_step)
    state = apply_walls(state, flags, fine_inflow, tile_rows, tile_cols)
    state = advance(state, fine_coef, fine_step)

    rows_sum = pair_matrix((coarse_rows, fine_rows), 0, fine_rows - 2)
    cols_sum = pair_matrix((fine_cols, coarse_cols), 1, fine_cols - 2)
    paired = matmul(rows_sum, jnp.concatenate([fine_coef, noise_height], axis=1))
    small = matmul(jnp.concatenate([paired[:, :fine_cols], paired[:, fine_cols:]], axis=0), cols_sum)
    coarse_coef = small[:coarse_rows] * 0.25
    depth = 1.0 + 0.1 * (small[coarse_rows:] * 0.25)
    coarse = (depth, 0.5 * depth, jnp.zeros_like(depth))
    coarse_inflow = jnp.broadcast_to(coarse_inflow_ref[...], COARSE_SHAPE)
    coarse = walls_at_rest(coarse, flags, coarse_inflow, out_rows, out_cols)
    coarse = advance_at_rest(coarse, coarse_coef, coarse_step)

    rows_out = pair_matrix((out_rows, tile_rows), 0, None)
    cols_out = pair_matrix((tile_cols, out_cols), 1, None)
    paired = matmul(
        rows_out, jnp.concatenate([values[:tile_rows, :tile_cols] for values in state], axis=1)
    )
    stacked = jnp.concatenate(
        [paired[:, field * tile_cols: (field + 1) * tile_cols] for field in range(3)], axis=0
    )
    means = matmul(stacked, cols_out)
    for field in range(3):
        mean = means[field * out_rows: (field + 1) * out_rows] * 0.25
        mean_ref[field] = mean
        corr_ref[field] = mean - coarse[field][:out_rows, :out_cols]


def body(friction, height, inflow):
    strip = lax.axis_index("col") * lax.axis_size("level") + lax.axis_index("level")
    strips = lax.axis_size("col") * lax.axis_size("level")
    row_index = lax.axis_index("row")
    flags = jnp.stack(
        [row_index == 0, row_index == lax.axis_size("row") - 1, strip == 0, strip == strips - 1]
    ).astype(jnp.int32)
    tile_rows, tile_cols = friction.shape[1], friction.shape[2]
    out_rows, out_cols = tile_rows // 2, tile_cols // 2

    noise = with_halo(jnp.concatenate([friction, height], axis=0))
    lead = FINE_SHAPE[0] - tile_rows - HALO
    fine_inflow = wrapped_rows(inflow, row_index * tile_rows, FINE_SHAPE[0], lead)
    lead = COARSE_SHAPE[0] - out_rows - 1
    coarse_inflow = wrapped_rows(pair_mean(inflow), row_index * out_rows, COARSE_SHAPE[0], lead)

    out = jax.ShapeDtypeStruct((3, out_rows, out_cols), jnp.float32)
    vmem = pl.BlockSpec(memory_space=pltpu.VMEM)
    mean, corr = pl.pallas_call(
        level_kernel,
        out_shape=(out, out),
        in_specs=[pl.BlockSpec(memory_space=pltpu.SMEM), vmem, vmem, vmem],
        out_specs=(vmem, vmem),
    )(flags, noise, fine_inflow, coarse_inflow)
    return (mean[None], corr[None])


def solution(mesh):
    in_specs = (P("level", "row", "col"), P("level", "row", "col"), P())
    out_specs = (P("level", None, "row", "col"), P("level", None, "row", "col"))
    return jax.shard_map(body, mesh=mesh, in_specs=in_specs, out_specs=out_specs, check_vma=False)
```

```python
import jax
import jax.numpy as jnp
from jax import lax
from jax.experimental import pallas as pl
from jax.experimental.pallas import tpu as pltpu
from jax.sharding import PartitionSpec as P

step_ratio = 0.15
fine_step = 0.15
coarse_step = 0.3
HALO = 2
FINE_SHAPE = (72, 384)
COARSE_SHAPE = (40, 256)


def pair_mean(values):
    paired = values.reshape(-1, 2)
    return (paired[:, 0] + paired[:, 1]) * 0.5


def swap_pairs(count, parity, place=lambda i: i):
    pairs = []
    for i in range(parity, count - 1, 2):
        pairs += [(place(i), place(i + 1)), (place(i + 1), place(i))]
    return pairs


def strip_place(strip):
    levels = lax.axis_size("level")
    return (strip % levels) * lax.axis_size("col") + strip // levels


def swapped(first, last, index, count, axis, place=lambda i: i):
    odd = index % 2 == 1
    got = []
    for parity in range(2):
        sends_last = odd if parity else jnp.logical_not(odd)
        block = jnp.where(sends_last, last, first)
        got.append(lax.ppermute(block, axis, swap_pairs(count, parity, place)))
    before = jnp.where(odd, got[0], got[1])
    after = jnp.where(odd, got[1], got[0])
    return before, after


def with_halo(noise):
    fields, count_rows, count_cols = noise.shape
    strips = lax.axis_size("col") * lax.axis_size("level")
    strip = lax.axis_index("col") * lax.axis_size("level") + lax.axis_index("level")
    row_index = lax.axis_index("row")
    rows = lax.axis_size("row")
    north, south = swapped(noise[:, :HALO], noise[:, -HALO:], row_index, rows, "row")
    west, east = swapped(
        noise[:, :, :HALO], noise[:, :, -HALO:], strip, strips, ("level", "col"), strip_place
    )
    sides = jnp.concatenate([west, east], axis=2)
    above, below = swapped(sides[:, :HALO], sides[:, -HALO:], row_index, rows, "row")
    gap_cols = FINE_SHAPE[1] - count_cols - 2 * HALO

    def band(middle, corners):
        gap = jnp.zeros(middle.shape[:2] + (gap_cols,), noise.dtype)
        return jnp.concatenate([middle, corners[:, :, HALO:], gap, corners[:, :, :HALO]], axis=2)

    gap_rows = FINE_SHAPE[0] - count_rows - 2 * HALO
    return jnp.concatenate(
        [
            band(noise, sides),
            band(south, below),
            jnp.zeros((fields, gap_rows, FINE_SHAPE[1]), noise.dtype),
            band(north, above),
        ],
        axis=1,
    )


def wrapped_rows(values, start, count, lead):
    padded = jnp.pad(values, lead)
    window = lax.dynamic_slice_in_dim(padded, start, count)
    return (0.5 + jnp.roll(window, -lead)).reshape(count, 1)


def next_of(values, axis):
    return pltpu.roll(values, values.shape[axis] - 1, axis)


def prev_of(values, axis):
    return pltpu.roll(values, 1, axis)


def apply_walls(state, flags, inflow_speed, bottom_row, right_col):
    depth, along_cols, along_rows = state
    shape = depth.shape
    row_at = lax.broadcasted_iota(jnp.int32, shape, 0)
    col_at = lax.broadcasted_iota(jnp.int32, shape, 1)
    top = jnp.logical_and(row_at == shape[0] - 1, flags[0] == 1)
    bottom = jnp.logical_and(row_at == bottom_row, flags[1] == 1)
    left = jnp.logical_and(col_at == shape[1] - 1, flags[2] == 1)
    right = jnp.logical_and(col_at == right_col, flags[3] == 1)

    def rows_fixed(values, sign):
        below = next_of(values, 0)
        above = prev_of(values, 0)
        if sign < 0:
            below = -below
            above = -above
        return jnp.where(top, below, jnp.where(bottom, above, values))

    depth = rows_fixed(depth, 1)
    along_cols = rows_fixed(along_cols, 1)
    along_rows = rows_fixed(along_rows, -1)
    source = next_of(depth, 1)
    entering = (source, source * inflow_speed, jnp.zeros_like(source))
    fixed = []
    for values, inflowing in zip((depth, along_cols, along_rows), entering):
        fixed.append(jnp.where(left, inflowing, jnp.where(right, prev_of(values, 1), values)))
    return tuple(fixed)


def face_flux(state, flux, speed, axis):
    reach = 0.5 * jnp.maximum(next_of(speed, axis), speed)
    return [
        0.5 * (next_of(f, axis) + f) - reach * (next_of(u, axis) - u)
        for f, u in zip(flux, state)
    ]


def advance(state, friction_coef, step):
    depth, along_cols, along_rows = state
    velocity = along_cols / depth
    flux = (along_cols, along_cols * velocity + 0.5 * depth * depth, along_rows * velocity)
    face_x = face_flux(state, flux, jnp.abs(velocity) + jnp.sqrt(depth), 1)
    velocity = along_rows / depth
    flux = (along_rows, along_cols * velocity, along_rows * velocity + 0.5 * depth * depth)
    face_y = face_flux(state, flux, jnp.abs(velocity) + jnp.sqrt(depth), 0)
    moved = [
        u - step_ratio * (fx - prev_of(fx, 1) + (fy - prev_of(fy, 0)))
        for u, fx, fy in zip(state, face_x, face_y)
    ]
    depth = moved[0]
    speed = jnp.sqrt(moved[1] * moved[1] + moved[2] * moved[2]) / depth
    damping = 1.0 / (1.0 + step * friction_coef * speed / depth)
    return (depth, moved[1] * damping, moved[2] * damping)


def walls_at_rest(state, flags, inflow_speed, bottom_row, right_col):
    depth, along_cols, _ = state
    depth, along_cols, _ = apply_walls(
        (depth, along_cols, depth), flags, inflow_speed, bottom_row, right_col
    )
    return (depth, along_cols, jnp.zeros_like(depth))


def advance_at_rest(state, friction_coef, step):
    depth, along_cols, _ = state
    velocity = along_cols / depth
    root = jnp.sqrt(depth)
    flux = (along_cols, along_cols * velocity + 0.5 * depth * depth)
    face_x = face_flux((depth, along_cols), flux, jnp.abs(velocity) + root, 1)
    reach = 0.5 * jnp.maximum(next_of(root, 0), root)
    face_y = [0.0 - reach * (next_of(u, 0) - u) for u in (depth, along_cols)]
    pressure = 0.5 * depth * depth
    pressure_face = 0.5 * (next_of(pressure, 0) + pressure)
    moved = [
        u - step_ratio * (fx - prev_of(fx, 1) + (fy - prev_of(fy, 0)))
        for u, fx, fy in zip((depth, along_cols), face_x, face_y)
    ]
    moved.append(0.0 - step_ratio * (pressure_face - prev_of(pressure_face, 0)))
    depth = moved[0]
    speed = jnp.sqrt(moved[1] * moved[1] + moved[2] * moved[2]) / depth
    damping = 1.0 / (1.0 + step * friction_coef * speed / depth)
    return (depth, moved[1] * damping, moved[2] * damping)


def pair_matrix(shape, out_axis, last_from):
    out_at = lax.broadcasted_iota(jnp.int32, shape, out_axis)
    in_at = lax.broadcasted_iota(jnp.int32, shape, 1 - out_axis)
    hit = jnp.right_shift(in_at, 1) == out_at
    if last_from is not None:
        last = shape[out_axis] - 1
        hit = jnp.logical_or(hit, jnp.logical_and(out_at == last, in_at >= last_from))
    return hit.astype(jnp.float32)


def matmul(a, b):
    return jnp.dot(a, b, precision=lax.Precision.HIGHEST, preferred_element_type=jnp.float32)


def level_kernel(flags_ref, noise_ref, fine_inflow_ref, coarse_inflow_ref, mean_ref, corr_ref):
    flags = [flags_ref[i] for i in range(4)]
    fine_rows, fine_cols = FINE_SHAPE
    coarse_rows, coarse_cols = COARSE_SHAPE
    out_rows, out_cols = mean_ref.shape[1], mean_ref.shape[2]
    tile_rows, tile_cols = 2 * out_rows, 2 * out_cols

    fine_coef = noise_ref[0]
    noise_height = noise_ref[1]
    depth = 1.0 + 0.1 * noise_height
    state = (depth, 0.5 * depth, jnp.zeros_like(depth))
    fine_inflow = jnp.broadcast_to(fine_inflow_ref[...], FINE_SHAPE)
    state = walls_at_rest(state, flags, fine_inflow, tile_rows, tile_cols)
    state = advance_at_rest(state, fine_coef, fine_step)
    state = apply_walls(state, flags, fine_inflow, tile_rows, tile_cols)
    state = advance(state, fine_coef, fine_step)

    rows_sum = pair_matrix((coarse_rows, fine_rows), 0, fine_rows - 2)
    cols_sum = pair_matrix((fine_cols, coarse_cols), 1, fine_cols - 2)
    paired = matmul(rows_sum, jnp.concatenate([fine_coef, noise_height], axis=1))
    small = matmul(jnp.concatenate([paired[:, :fine_cols], paired[:, fine_cols:]], axis=0), cols_sum)
    coarse_coef = small[:coarse_rows] * 0.25
    depth = 1.0 + 0.1 * (small[coarse_rows:] * 0.25)
    coarse = (depth, 0.5 * depth, jnp.zeros_like(depth))
    coarse_inflow = jnp.broadcast_to(coarse_inflow_ref[...], COARSE_SHAPE)
    coarse = walls_at_rest(coarse, flags, coarse_inflow, out_rows, out_cols)
    coarse = advance_at_rest(coarse, coarse_coef, coarse_step)

    rows_out = pair_matrix((out_rows, tile_rows), 0, None)
    cols_out = pair_matrix((tile_cols, out_cols), 1, None)
    paired = matmul(
        rows_out, jnp.concatenate([values[:tile_rows, :tile_cols] for values in state], axis=1)
    )
    stacked = jnp.concatenate(
        [paired[:, field * tile_cols: (field + 1) * tile_cols] for field in range(3)], axis=0
    )
    means = matmul(stacked, cols_out)
    for field in range(3):
        mean = means[field * out_rows: (field + 1) * out_rows] * 0.25
        mean_ref[field] = mean
        corr_ref[field] = mean - coarse[field][:out_rows, :out_cols]


def body(friction, height, inflow):
    strip = lax.axis_index("col") * lax.axis_size("level") + lax.axis_index("level")
    strips = lax.axis_size("col") * lax.axis_size("level")
    row_index = lax.axis_index("row")
    flags = jnp.stack(
        [row_index == 0, row_index == lax.axis_size("row") - 1, strip == 0, strip == strips - 1]
    ).astype(jnp.int32)
    tile_rows, tile_cols = friction.shape[1], friction.shape[2]
    out_rows, out_cols = tile_rows // 2, tile_cols // 2

    noise = with_halo(jnp.concatenate([friction, height], axis=0))
    lead = FINE_SHAPE[0] - tile_rows - HALO
    fine_inflow = wrapped_rows(inflow, row_index * tile_rows, FINE_SHAPE[0], lead)
    lead = COARSE_SHAPE[0] - out_rows - 1
    coarse_inflow = wrapped_rows(pair_mean(inflow), row_index * out_rows, COARSE_SHAPE[0], lead)

    out = jax.ShapeDtypeStruct((3, out_rows, out_cols), jnp.float32)
    vmem = pl.BlockSpec(memory_space=pltpu.VMEM)
    mean, corr = pl.pallas_call(
        level_kernel,
        out_shape=(out, out),
        in_specs=[pl.BlockSpec(memory_space=pltpu.SMEM), vmem, vmem, vmem],
        out_specs=(vmem, vmem),
    )(flags, noise, fine_inflow, coarse_inflow)
    return (mean[None], corr[None])


def solution(mesh):
    in_specs = (P("level", "row", "col"), P("level", "row", "col"), P())
    out_specs = (P("level", None, "row", "col"), P("level", None, "row", "col"))
    return jax.shard_map(body, mesh=mesh, in_specs=in_specs, out_specs=out_specs, check_vma=False)
```

```python
import jax
import jax.numpy as jnp
from jax import lax
from jax.experimental import pallas as pl
from jax.experimental.pallas import tpu as pltpu
from jax.sharding import PartitionSpec as P

step_ratio = 0.15
fine_step = 0.15
coarse_step = 0.3
HALO = 2
FINE_SHAPE = (72, 384)
COARSE_SHAPE = (40, 256)


def pair_mean(values):
    paired = values.reshape(-1, 2)
    return (paired[:, 0] + paired[:, 1]) * 0.5


def swap_pairs(count, parity, place=lambda i: i):
    pairs = []
    for i in range(parity, count - 1, 2):
        pairs += [(place(i), place(i + 1)), (place(i + 1), place(i))]
    return pairs


def strip_place(strip):
    levels = lax.axis_size("level")
    return (strip % levels) * lax.axis_size("col") + strip // levels


def swapped(first, last, index, count, axis, place=lambda i: i):
    odd = index % 2 == 1
    got = []
    for parity in range(2):
        sends_last = odd if parity else jnp.logical_not(odd)
        block = jnp.where(sends_last, last, first)
        got.append(lax.ppermute(block, axis, swap_pairs(count, parity, place)))
    before = jnp.where(odd, got[0], got[1])
    after = jnp.where(odd, got[1], got[0])
    return before, after


def swap_once(first, last, index, count, axis, parity, place=lambda i: i):
    gets_after = (index % 2 == 1) if parity else (index % 2 == 0)
    block = jnp.where(gets_after, last, first)
    return gets_after, lax.ppermute(block, axis, swap_pairs(count, parity, place))


def with_halo(noise):
    fields, count_rows, count_cols = noise.shape
    strips = lax.axis_size("col") * lax.axis_size("level")
    strip = lax.axis_index("col") * lax.axis_size("level") + lax.axis_index("level")
    across = ("level", "col")
    gap_cols = FINE_SHAPE[1] - count_cols - 2 * HALO

    def sides(width, after, before):
        gap = jnp.zeros((fields, width, gap_cols), noise.dtype)
        return [after, gap, before]

    gets_after, got = swap_once(
        noise[:, :, :HALO], noise[:, :, -HALO:], strip, strips, across, 1, strip_place
    )
    none = jnp.zeros_like(got)
    wide = jnp.concatenate(
        [noise] + sides(count_rows, jnp.where(gets_after, got, none),
                        jnp.where(gets_after, none, got)),
        axis=2,
    )
    north, south = swapped(
        wide[:, :HALO], wide[:, -HALO:], lax.axis_index("row"), lax.axis_size("row"), "row"
    )
    gap_rows = FINE_SHAPE[0] - count_rows - 2 * HALO
    tall = jnp.concatenate(
        [wide, south, jnp.zeros((fields, gap_rows, FINE_SHAPE[1]), noise.dtype), north], axis=1
    )
    gets_after, got = swap_once(
        tall[:, :, :HALO], tall[:, :, count_cols - HALO: count_cols], strip, strips, across, 0,
        strip_place,
    )
    east = tall[:, :, count_cols: count_cols + HALO]
    west = tall[:, :, FINE_SHAPE[1] - HALO:]
    return jnp.concatenate(
        [tall[:, :, :count_cols]]
        + sides(FINE_SHAPE[0], jnp.where(gets_after, got, east), jnp.where(gets_after, west, got)),
        axis=2,
    )


def wrapped_rows(values, start, count, lead):
    padded = jnp.pad(values, lead)
    window = lax.dynamic_slice_in_dim(padded, start, count)
    return (0.5 + jnp.roll(window, -lead)).reshape(count, 1)


def next_of(values, axis):
    return pltpu.roll(values, values.shape[axis] - 1, axis)


def prev_of(values, axis):
    return pltpu.roll(values, 1, axis)


def apply_walls(state, flags, inflow_speed, bottom_row, right_col):
    depth, along_cols, along_rows = state
    shape = depth.shape
    row_at = lax.broadcasted_iota(jnp.int32, shape, 0)
    col_at = lax.broadcasted_iota(jnp.int32, shape, 1)
    top = jnp.logical_and(row_at == shape[0] - 1, flags[0] == 1)
    bottom = jnp.logical_and(row_at == bottom_row, flags[1] == 1)
    left = jnp.logical_and(col_at == shape[1] - 1, flags[2] == 1)
    right = jnp.logical_and(col_at == right_col, flags[3] == 1)

    def rows_fixed(values, sign):
        below = next_of(values, 0)
        above = prev_of(values, 0)
        if sign < 0:
            below = -below
            above = -above
        return jnp.where(top, below, jnp.where(bottom, above, values))

    depth = rows_fixed(depth, 1)
    along_cols = rows_fixed(along_cols, 1)
    along_rows = rows_fixed(along_rows, -1)
    source = next_of(depth, 1)
    entering = (source, source * inflow_speed, jnp.zeros_like(source))
    fixed = []
    for values, inflowing in zip((depth, along_cols, along_rows), entering):
        fixed.append(jnp.where(left, inflowing, jnp.where(right, prev_of(values, 1), values)))
    return tuple(fixed)


def face_flux(state, flux, speed, axis):
    reach = 0.5 * jnp.maximum(next_of(speed, axis), speed)
    return [
        0.5 * (next_of(f, axis) + f) - reach * (next_of(u, axis) - u)
        for f, u in zip(flux, state)
    ]


def advance(state, friction_coef, step):
    depth, along_cols, along_rows = state
    velocity = along_cols / depth
    flux = (along_cols, along_cols * velocity + 0.5 * depth * depth, along_rows * velocity)
    face_x = face_flux(state, flux, jnp.abs(velocity) + jnp.sqrt(depth), 1)
    velocity = along_rows / depth
    flux = (along_rows, along_cols * velocity, along_rows * velocity + 0.5 * depth * depth)
    face_y = face_flux(state, flux, jnp.abs(velocity) + jnp.sqrt(depth), 0)
    moved = [
        u - step_ratio * (fx - prev_of(fx, 1) + (fy - prev_of(fy, 0)))
        for u, fx, fy in zip(state, face_x, face_y)
    ]
    depth = moved[0]
    speed = jnp.sqrt(moved[1] * moved[1] + moved[2] * moved[2]) / depth
    damping = 1.0 / (1.0 + step * friction_coef * speed / depth)
    return (depth, moved[1] * damping, moved[2] * damping)


def walls_at_rest(state, flags, inflow_speed, bottom_row, right_col):
    depth, along_cols, _ = state
    depth, along_cols, _ = apply_walls(
        (depth, along_cols, depth), flags, inflow_speed, bottom_row, right_col
    )
    return (depth, along_cols, jnp.zeros_like(depth))


def advance_at_rest(state, friction_coef, step):
    depth, along_cols, _ = state
    velocity = along_cols / depth
    root = jnp.sqrt(depth)
    flux = (along_cols, along_cols * velocity + 0.5 * depth * depth)
    face_x = face_flux((depth, along_cols), flux, jnp.abs(velocity) + root, 1)
    reach = 0.5 * jnp.maximum(next_of(root, 0), root)
    face_y = [0.0 - reach * (next_of(u, 0) - u) for u in (depth, along_cols)]
    pressure = 0.5 * depth * depth
    pressure_face = 0.5 * (next_of(pressure, 0) + pressure)
    moved = [
        u - step_ratio * (fx - prev_of(fx, 1) + (fy - prev_of(fy, 0)))
        for u, fx, fy in zip((depth, along_cols), face_x, face_y)
    ]
    moved.append(0.0 - step_ratio * (pressure_face - prev_of(pressure_face, 0)))
    depth = moved[0]
    speed = jnp.sqrt(moved[1] * moved[1] + moved[2] * moved[2]) / depth
    damping = 1.0 / (1.0 + step * friction_coef * speed / depth)
    return (depth, moved[1] * damping, moved[2] * damping)


def pair_matrix(shape, out_axis, last_from):
    out_at = lax.broadcasted_iota(jnp.int32, shape, out_axis)
    in_at = lax.broadcasted_iota(jnp.int32, shape, 1 - out_axis)
    hit = jnp.right_shift(in_at, 1) == out_at
    if last_from is not None:
        last = shape[out_axis] - 1
        hit = jnp.logical_or(hit, jnp.logical_and(out_at == last, in_at >= last_from))
    return hit.astype(jnp.float32)


def matmul(a, b):
    return jnp.dot(a, b, precision=lax.Precision.HIGHEST, preferred_element_type=jnp.float32)


def level_kernel(flags_ref, noise_ref, fine_inflow_ref, coarse_inflow_ref, mean_ref, corr_ref):
    flags = [flags_ref[i] for i in range(4)]
    fine_rows, fine_cols = FINE_SHAPE
    coarse_rows, coarse_cols = COARSE_SHAPE
    out_rows, out_cols = mean_ref.shape[1], mean_ref.shape[2]
    tile_rows, tile_cols = 2 * out_rows, 2 * out_cols

    fine_coef = noise_ref[0]
    noise_height = noise_ref[1]
    depth = 1.0 + 0.1 * noise_height
    state = (depth, 0.5 * depth, jnp.zeros_like(depth))
    fine_inflow = jnp.broadcast_to(fine_inflow_ref[...], FINE_SHAPE)
    state = walls_at_rest(state, flags, fine_inflow, tile_rows, tile_cols)
    state = advance_at_rest(state, fine_coef, fine_step)
    state = apply_walls(state, flags, fine_inflow, tile_rows, tile_cols)
    state = advance(state, fine_coef, fine_step)

    rows_sum = pair_matrix((coarse_rows, fine_rows), 0, fine_rows - 2)
    cols_sum = pair_matrix((fine_cols, coarse_cols), 1, fine_cols - 2)
    paired = matmul(rows_sum, jnp.concatenate([fine_coef, noise_height], axis=1))
    small = matmul(jnp.concatenate([paired[:, :fine_cols], paired[:, fine_cols:]], axis=0), cols_sum)
    coarse_coef = small[:coarse_rows] * 0.25
    depth = 1.0 + 0.1 * (small[coarse_rows:] * 0.25)
    coarse = (depth, 0.5 * depth, jnp.zeros_like(depth))
    coarse_inflow = jnp.broadcast_to(coarse_inflow_ref[...], COARSE_SHAPE)
    coarse = walls_at_rest(coarse, flags, coarse_inflow, out_rows, out_cols)
    coarse = advance_at_rest(coarse, coarse_coef, coarse_step)

    rows_out = pair_matrix((out_rows, tile_rows), 0, None)
    cols_out = pair_matrix((tile_cols, out_cols), 1, None)
    paired = matmul(
        rows_out, jnp.concatenate([values[:tile_rows, :tile_cols] for values in state], axis=1)
    )
    stacked = jnp.concatenate(
        [paired[:, field * tile_cols: (field + 1) * tile_cols] for field in range(3)], axis=0
    )
    means = matmul(stacked, cols_out)
    for field in range(3):
        mean = means[field * out_rows: (field + 1) * out_rows] * 0.25
        mean_ref[field] = mean
        corr_ref[field] = mean - coarse[field][:out_rows, :out_cols]


def body(friction, height, inflow):
    strip = lax.axis_index("col") * lax.axis_size("level") + lax.axis_index("level")
    strips = lax.axis_size("col") * lax.axis_size("level")
    row_index = lax.axis_index("row")
    flags = jnp.stack(
        [row_index == 0, row_index == lax.axis_size("row") - 1, strip == 0, strip == strips - 1]
    ).astype(jnp.int32)
    tile_rows, tile_cols = friction.shape[1], friction.shape[2]
    out_rows, out_cols = tile_rows // 2, tile_cols // 2

    noise = with_halo(jnp.concatenate([friction, height], axis=0))
    lead = FINE_SHAPE[0] - tile_rows - HALO
    fine_inflow = wrapped_rows(inflow, row_index * tile_rows, FINE_SHAPE[0], lead)
    lead = COARSE_SHAPE[0] - out_rows - 1
    coarse_inflow = wrapped_rows(pair_mean(inflow), row_index * out_rows, COARSE_SHAPE[0], lead)

    out = jax.ShapeDtypeStruct((3, out_rows, out_cols), jnp.float32)
    vmem = pl.BlockSpec(memory_space=pltpu.VMEM)
    mean, corr = pl.pallas_call(
        level_kernel,
        out_shape=(out, out),
        in_specs=[pl.BlockSpec(memory_space=pltpu.SMEM), vmem, vmem, vmem],
        out_specs=(vmem, vmem),
    )(flags, noise, fine_inflow, coarse_inflow)
    return (mean[None], corr[None])


def solution(mesh):
    in_specs = (P("level", "row", "col"), P("level", "row", "col"), P())
    out_specs = (P("level", None, "row", "col"), P("level", None, "row", "col"))
    return jax.shard_map(body, mesh=mesh, in_specs=in_specs, out_specs=out_specs, check_vma=False)
```

```python
import jax
import jax.numpy as jnp
from jax import lax
from jax.experimental import pallas as pl
from jax.experimental.pallas import tpu as pltpu
from jax.sharding import PartitionSpec as P

step_ratio = 0.15
fine_step = 0.15
coarse_step = 0.3
HALO = 2
FINE_SHAPE = (72, 384)
COARSE_SHAPE = (40, 256)


def pair_mean(values):
    paired = values.reshape(-1, 2)
    return (paired[:, 0] + paired[:, 1]) * 0.5


def swap_pairs(count, parity, place=lambda i: i):
    pairs = []
    for i in range(parity, count - 1, 2):
        pairs += [(place(i), place(i + 1)), (place(i + 1), place(i))]
    return pairs


def strip_place(strip):
    levels = lax.axis_size("level")
    return (strip % levels) * lax.axis_size("col") + strip // levels


def swapped(first, last, index, count, axis, place=lambda i: i):
    odd = index % 2 == 1
    got = []
    for parity in range(2):
        sends_last = odd if parity else jnp.logical_not(odd)
        block = jnp.where(sends_last, last, first)
        got.append(lax.ppermute(block, axis, swap_pairs(count, parity, place)))
    before = jnp.where(odd, got[0], got[1])
    after = jnp.where(odd, got[1], got[0])
    return before, after


def with_halo(noise):
    fields, count_rows, count_cols = noise.shape
    strips = lax.axis_size("col") * lax.axis_size("level")
    strip = lax.axis_index("col") * lax.axis_size("level") + lax.axis_index("level")
    rows = lax.axis_size("row")
    north, south = swapped(
        noise[:, :HALO], noise[:, -HALO:], lax.axis_index("row"), rows, "row"
    )
    gap_rows = FINE_SHAPE[0] - count_rows - 2 * HALO
    tall = jnp.concatenate(
        [noise, south, jnp.zeros((fields, gap_rows, count_cols), noise.dtype), north], axis=1
    )
    west, east = swapped(
        tall[:, :, :HALO], tall[:, :, -HALO:], strip, strips, ("level", "col"), strip_place
    )
    gap_cols = FINE_SHAPE[1] - count_cols - 2 * HALO
    return jnp.concatenate(
        [tall, east, jnp.zeros((fields, FINE_SHAPE[0], gap_cols), noise.dtype), west], axis=2
    )


def wrapped_rows(values, start, count, lead):
    padded = jnp.pad(values, lead)
    window = lax.dynamic_slice_in_dim(padded, start, count)
    return (0.5 + jnp.roll(window, -lead)).reshape(count, 1)


def next_of(values, axis):
    return pltpu.roll(values, values.shape[axis] - 1, axis)


def prev_of(values, axis):
    return pltpu.roll(values, 1, axis)


def apply_walls(state, flags, inflow_speed, bottom_row, right_col):
    depth, along_cols, along_rows = state
    shape = depth.shape
    row_at = lax.broadcasted_iota(jnp.int32, shape, 0)
    col_at = lax.broadcasted_iota(jnp.int32, shape, 1)
    top = jnp.logical_and(row_at == shape[0] - 1, flags[0] == 1)
    bottom = jnp.logical_and(row_at == bottom_row, flags[1] == 1)
    left = jnp.logical_and(col_at == shape[1] - 1, flags[2] == 1)
    right = jnp.logical_and(col_at == right_col, flags[3] == 1)

    def rows_fixed(values, sign):
        below = next_of(values, 0)
        above = prev_of(values, 0)
        if sign < 0:
            below = -below
            above = -above
        return jnp.where(top, below, jnp.where(bottom, above, values))

    depth = rows_fixed(depth, 1)
    along_cols = rows_fixed(along_cols, 1)
    along_rows = rows_fixed(along_rows, -1)
    source = next_of(depth, 1)
    entering = (source, source * inflow_speed, jnp.zeros_like(source))
    fixed = []
    for values, inflowing in zip((depth, along_cols, along_rows), entering):
        fixed.append(jnp.where(left, inflowing, jnp.where(right, prev_of(values, 1), values)))
    return tuple(fixed)


def face_flux(state, flux, speed, axis):
    reach = 0.5 * jnp.maximum(next_of(speed, axis), speed)
    return [
        0.5 * (next_of(f, axis) + f) - reach * (next_of(u, axis) - u)
        for f, u in zip(flux, state)
    ]


def advance(state, friction_coef, step):
    depth, along_cols, along_rows = state
    inverse = 1.0 / depth
    velocity = along_cols * inverse
    flux = (along_cols, along_cols * velocity + 0.5 * depth * depth, along_rows * velocity)
    face_x = face_flux(state, flux, jnp.abs(velocity) + jnp.sqrt(depth), 1)
    velocity = along_rows * inverse
    flux = (along_rows, along_cols * velocity, along_rows * velocity + 0.5 * depth * depth)
    face_y = face_flux(state, flux, jnp.abs(velocity) + jnp.sqrt(depth), 0)
    moved = [
        u - step_ratio * (fx - prev_of(fx, 1) + (fy - prev_of(fy, 0)))
        for u, fx, fy in zip(state, face_x, face_y)
    ]
    depth = moved[0]
    inverse = 1.0 / depth
    speed = jnp.sqrt(moved[1] * moved[1] + moved[2] * moved[2]) * inverse
    damping = 1.0 / (1.0 + step * friction_coef * speed * inverse)
    return (depth, moved[1] * damping, moved[2] * damping)


def walls_at_rest(state, flags, inflow_speed, bottom_row, right_col):
    depth, along_cols, _ = state
    depth, along_cols, _ = apply_walls(
        (depth, along_cols, depth), flags, inflow_speed, bottom_row, right_col
    )
    return (depth, along_cols, jnp.zeros_like(depth))


def advance_at_rest(state, friction_coef, step):
    depth, along_cols, _ = state
    velocity = along_cols * (1.0 / depth)
    root = jnp.sqrt(depth)
    flux = (along_cols, along_cols * velocity + 0.5 * depth * depth)
    face_x = face_flux((depth, along_cols), flux, jnp.abs(velocity) + root, 1)
    reach = 0.5 * jnp.maximum(next_of(root, 0), root)
    face_y = [0.0 - reach * (next_of(u, 0) - u) for u in (depth, along_cols)]
    pressure = 0.5 * depth * depth
    pressure_face = 0.5 * (next_of(pressure, 0) + pressure)
    moved = [
        u - step_ratio * (fx - prev_of(fx, 1) + (fy - prev_of(fy, 0)))
        for u, fx, fy in zip((depth, along_cols), face_x, face_y)
    ]
    moved.append(0.0 - step_ratio * (pressure_face - prev_of(pressure_face, 0)))
    depth = moved[0]
    inverse = 1.0 / depth
    speed = jnp.sqrt(moved[1] * moved[1] + moved[2] * moved[2]) * inverse
    damping = 1.0 / (1.0 + step * friction_coef * speed * inverse)
    return (depth, moved[1] * damping, moved[2] * damping)


def pair_matrix(shape, out_axis, last_from):
    out_at = lax.broadcasted_iota(jnp.int32, shape, out_axis)
    in_at = lax.broadcasted_iota(jnp.int32, shape, 1 - out_axis)
    hit = jnp.right_shift(in_at, 1) == out_at
    if last_from is not None:
        last = shape[out_axis] - 1
        hit = jnp.logical_or(hit, jnp.logical_and(out_at == last, in_at >= last_from))
    return hit.astype(jnp.float32)


def matmul(a, b):
    return jnp.dot(a, b, precision=lax.Precision.HIGHEST, preferred_element_type=jnp.float32)


def level_kernel(flags_ref, noise_ref, fine_inflow_ref, coarse_inflow_ref, mean_ref, corr_ref):
    flags = [flags_ref[i] for i in range(4)]
    fine_rows, fine_cols = FINE_SHAPE
    coarse_rows, coarse_cols = COARSE_SHAPE
    out_rows, out_cols = mean_ref.shape[1], mean_ref.shape[2]
    tile_rows, tile_cols = 2 * out_rows, 2 * out_cols

    fine_coef = noise_ref[0]
    noise_height = noise_ref[1]
    depth = 1.0 + 0.1 * noise_height
    state = (depth, 0.5 * depth, jnp.zeros_like(depth))
    fine_inflow = jnp.broadcast_to(fine_inflow_ref[...], FINE_SHAPE)
    state = walls_at_rest(state, flags, fine_inflow, tile_rows, tile_cols)
    state = advance_at_rest(state, fine_coef, fine_step)
    state = apply_walls(state, flags, fine_inflow, tile_rows, tile_cols)
    state = advance(state, fine_coef, fine_step)

    rows_sum = pair_matrix((coarse_rows, fine_rows), 0, fine_rows - 2)
    cols_sum = pair_matrix((fine_cols, coarse_cols), 1, fine_cols - 2)
    paired = matmul(rows_sum, jnp.concatenate([fine_coef, noise_height], axis=1))
    small = matmul(jnp.concatenate([paired[:, :fine_cols], paired[:, fine_cols:]], axis=0), cols_sum)
    coarse_coef = small[:coarse_rows] * 0.25
    depth = 1.0 + 0.1 * (small[coarse_rows:] * 0.25)
    coarse = (depth, 0.5 * depth, jnp.zeros_like(depth))
    coarse_inflow = jnp.broadcast_to(coarse_inflow_ref[...], COARSE_SHAPE)
    coarse = walls_at_rest(coarse, flags, coarse_inflow, out_rows, out_cols)
    coarse = advance_at_rest(coarse, coarse_coef, coarse_step)

    rows_out = pair_matrix((out_rows, tile_rows), 0, None)
    cols_out = pair_matrix((tile_cols, out_cols), 1, None)
    paired = matmul(
        rows_out, jnp.concatenate([values[:tile_rows, :tile_cols] for values in state], axis=1)
    )
    stacked = jnp.concatenate(
        [paired[:, field * tile_cols: (field + 1) * tile_cols] for field in range(3)], axis=0
    )
    means = matmul(stacked, cols_out)
    for field in range(3):
        mean = means[field * out_rows: (field + 1) * out_rows] * 0.25
        mean_ref[field] = mean
        corr_ref[field] = mean - coarse[field][:out_rows, :out_cols]


def body(friction, height, inflow):
    strip = lax.axis_index("col") * lax.axis_size("level") + lax.axis_index("level")
    strips = lax.axis_size("col") * lax.axis_size("level")
    row_index = lax.axis_index("row")
    flags = jnp.stack(
        [row_index == 0, row_index == lax.axis_size("row") - 1, strip == 0, strip == strips - 1]
    ).astype(jnp.int32)
    tile_rows, tile_cols = friction.shape[1], friction.shape[2]
    out_rows, out_cols = tile_rows // 2, tile_cols // 2

    noise = with_halo(jnp.concatenate([friction, height], axis=0))
    lead = FINE_SHAPE[0] - tile_rows - HALO
    fine_inflow = wrapped_rows(inflow, row_index * tile_rows, FINE_SHAPE[0], lead)
    lead = COARSE_SHAPE[0] - out_rows - 1
    coarse_inflow = wrapped_rows(pair_mean(inflow), row_index * out_rows, COARSE_SHAPE[0], lead)

    out = jax.ShapeDtypeStruct((3, out_rows, out_cols), jnp.float32)
    vmem = pl.BlockSpec(memory_space=pltpu.VMEM)
    mean, corr = pl.pallas_call(
        level_kernel,
        out_shape=(out, out),
        in_specs=[pl.BlockSpec(memory_space=pltpu.SMEM), vmem, vmem, vmem],
        out_specs=(vmem, vmem),
    )(flags, noise, fine_inflow, coarse_inflow)
    return (mean[None], corr[None])


def solution(mesh):
    in_specs = (P("level", "row", "col"), P("level", "row", "col"), P())
    out_specs = (P("level", None, "row", "col"), P("level", None, "row", "col"))
    return jax.shard_map(body, mesh=mesh, in_specs=in_specs, out_specs=out_specs, check_vma=False)
```

```python
import jax
import jax.numpy as jnp
from jax import lax
from jax.experimental import pallas as pl
from jax.experimental.pallas import tpu as pltpu
from jax.sharding import PartitionSpec as P

step_ratio = 0.15
fine_step = 0.15
coarse_step = 0.3
HALO = 2
FINE_SHAPE = (72, 384)
COARSE_SHAPE = (40, 256)


def pair_mean(values):
    paired = values.reshape(-1, 2)
    return (paired[:, 0] + paired[:, 1]) * 0.5


def swap_pairs(count, parity, place=lambda i: i):
    pairs = []
    for i in range(parity, count - 1, 2):
        pairs += [(place(i), place(i + 1)), (place(i + 1), place(i))]
    return pairs


def strip_place(strip):
    levels = lax.axis_size("level")
    return (strip % levels) * lax.axis_size("col") + strip // levels


def swapped(first, last, index, count, axis, place=lambda i: i):
    odd = index % 2 == 1
    got = []
    for parity in range(2):
        sends_last = odd if parity else jnp.logical_not(odd)
        block = jnp.where(sends_last, last, first)
        got.append(lax.ppermute(block, axis, swap_pairs(count, parity, place)))
    before = jnp.where(odd, got[0], got[1])
    after = jnp.where(odd, got[1], got[0])
    return before, after


def with_halo(noise):
    fields, count_rows, count_cols = noise.shape
    strips = lax.axis_size("col") * lax.axis_size("level")
    strip = lax.axis_index("col") * lax.axis_size("level") + lax.axis_index("level")
    rows = lax.axis_size("row")
    north, south = swapped(
        noise[:, :HALO], noise[:, -HALO:], lax.axis_index("row"), rows, "row"
    )
    gap_rows = FINE_SHAPE[0] - count_rows - 2 * HALO
    tall = jnp.concatenate(
        [noise, south, jnp.zeros((fields, gap_rows, count_cols), noise.dtype), north], axis=1
    )
    west, east = swapped(
        tall[:, :, :HALO], tall[:, :, -HALO:], strip, strips, ("level", "col"), strip_place
    )
    return tall, west, east


def wrapped_rows(values, start, count, lead):
    padded = jnp.pad(values, lead)
    window = lax.dynamic_slice_in_dim(padded, start, count)
    return (0.5 + jnp.roll(window, -lead)).reshape(count, 1)


def next_of(values, axis):
    return pltpu.roll(values, values.shape[axis] - 1, axis)


def prev_of(values, axis):
    return pltpu.roll(values, 1, axis)


def apply_walls(state, flags, inflow_speed, bottom_row, right_col, left_col=-1):
    depth, along_cols, along_rows = state
    shape = depth.shape
    row_at = lax.broadcasted_iota(jnp.int32, shape, 0)
    col_at = lax.broadcasted_iota(jnp.int32, shape, 1)
    top = jnp.logical_and(row_at == shape[0] - 1, flags[0] == 1)
    bottom = jnp.logical_and(row_at == bottom_row, flags[1] == 1)
    left = jnp.logical_and(col_at == left_col % shape[1], flags[2] == 1)
    right = jnp.logical_and(col_at == right_col, flags[3] == 1)

    def rows_fixed(values, sign):
        below = next_of(values, 0)
        above = prev_of(values, 0)
        if sign < 0:
            below = -below
            above = -above
        return jnp.where(top, below, jnp.where(bottom, above, values))

    depth = rows_fixed(depth, 1)
    along_cols = rows_fixed(along_cols, 1)
    along_rows = rows_fixed(along_rows, -1)
    source = next_of(depth, 1)
    entering = (source, source * inflow_speed, jnp.zeros_like(source))
    fixed = []
    for values, inflowing in zip((depth, along_cols, along_rows), entering):
        fixed.append(jnp.where(left, inflowing, jnp.where(right, prev_of(values, 1), values)))
    return tuple(fixed)


def face_flux(state, flux, speed, axis):
    reach = 0.5 * jnp.maximum(next_of(speed, axis), speed)
    return [
        0.5 * (next_of(f, axis) + f) - reach * (next_of(u, axis) - u)
        for f, u in zip(flux, state)
    ]


def advance(state, friction_coef, step):
    depth, along_cols, along_rows = state
    inverse = 1.0 / depth
    velocity = along_cols * inverse
    flux = (along_cols, along_cols * velocity + 0.5 * depth * depth, along_rows * velocity)
    face_x = face_flux(state, flux, jnp.abs(velocity) + jnp.sqrt(depth), 1)
    velocity = along_rows * inverse
    flux = (along_rows, along_cols * velocity, along_rows * velocity + 0.5 * depth * depth)
    face_y = face_flux(state, flux, jnp.abs(velocity) + jnp.sqrt(depth), 0)
    moved = [
        u - step_ratio * (fx - prev_of(fx, 1) + (fy - prev_of(fy, 0)))
        for u, fx, fy in zip(state, face_x, face_y)
    ]
    depth = moved[0]
    inverse = 1.0 / depth
    speed = jnp.sqrt(moved[1] * moved[1] + moved[2] * moved[2]) * inverse
    damping = 1.0 / (1.0 + step * friction_coef * speed * inverse)
    return (depth, moved[1] * damping, moved[2] * damping)


def walls_at_rest(state, flags, inflow_speed, bottom_row, right_col, left_col=-1):
    depth, along_cols, _ = state
    depth, along_cols, _ = apply_walls(
        (depth, along_cols, depth), flags, inflow_speed, bottom_row, right_col, left_col
    )
    return (depth, along_cols, jnp.zeros_like(depth))


def advance_at_rest(state, friction_coef, step):
    depth, along_cols, _ = state
    velocity = along_cols * (1.0 / depth)
    root = jnp.sqrt(depth)
    flux = (along_cols, along_cols * velocity + 0.5 * depth * depth)
    face_x = face_flux((depth, along_cols), flux, jnp.abs(velocity) + root, 1)
    reach = 0.5 * jnp.maximum(next_of(root, 0), root)
    face_y = [0.0 - reach * (next_of(u, 0) - u) for u in (depth, along_cols)]
    pressure = 0.5 * depth * depth
    pressure_face = 0.5 * (next_of(pressure, 0) + pressure)
    moved = [
        u - step_ratio * (fx - prev_of(fx, 1) + (fy - prev_of(fy, 0)))
        for u, fx, fy in zip((depth, along_cols), face_x, face_y)
    ]
    moved.append(0.0 - step_ratio * (pressure_face - prev_of(pressure_face, 0)))
    depth = moved[0]
    inverse = 1.0 / depth
    speed = jnp.sqrt(moved[1] * moved[1] + moved[2] * moved[2]) * inverse
    damping = 1.0 / (1.0 + step * friction_coef * speed * inverse)
    return (depth, moved[1] * damping, moved[2] * damping)


def pair_matrix(shape, out_axis, last_from):
    out_at = lax.broadcasted_iota(jnp.int32, shape, out_axis)
    in_at = lax.broadcasted_iota(jnp.int32, shape, 1 - out_axis)
    hit = jnp.right_shift(in_at, 1) == out_at
    if last_from is not None:
        last = shape[out_axis] - 1
        hit = jnp.logical_or(hit, jnp.logical_and(out_at == last, in_at >= last_from))
    return hit.astype(jnp.float32)


def matmul(a, b):
    return jnp.dot(a, b, precision=lax.Precision.HIGHEST, preferred_element_type=jnp.float32)


def level_kernel(flags_ref, noise_ref, fine_inflow_ref, coarse_inflow_ref, mean_ref, corr_ref):
    flags = [flags_ref[i] for i in range(4)]
    fine_rows, fine_cols = FINE_SHAPE
    coarse_rows, coarse_cols = COARSE_SHAPE
    out_rows, out_cols = mean_ref.shape[1], mean_ref.shape[2]
    tile_rows, tile_cols = 2 * out_rows, 2 * out_cols

    fine_coef = noise_ref[0]
    noise_height = noise_ref[1]
    depth = 1.0 + 0.1 * noise_height
    state = (depth, 0.5 * depth, jnp.zeros_like(depth))
    fine_inflow = jnp.broadcast_to(fine_inflow_ref[...], FINE_SHAPE)
    state = walls_at_rest(state, flags, fine_inflow, tile_rows, tile_cols)
    state = advance_at_rest(state, fine_coef, fine_step)
    state = apply_walls(state, flags, fine_inflow, tile_rows, tile_cols)
    state = advance(state, fine_coef, fine_step)

    rows_sum = pair_matrix((coarse_rows, fine_rows), 0, fine_rows - 2)
    cols_sum = pair_matrix((fine_cols, coarse_cols), 1, fine_cols - 2)
    paired = matmul(rows_sum, jnp.concatenate([fine_coef, noise_height], axis=1))
    small = matmul(jnp.concatenate([paired[:, :fine_cols], paired[:, fine_cols:]], axis=0), cols_sum)
    coarse_coef = small[:coarse_rows] * 0.25
    depth = 1.0 + 0.1 * (small[coarse_rows:] * 0.25)
    coarse = (depth, 0.5 * depth, jnp.zeros_like(depth))
    coarse_inflow = jnp.broadcast_to(coarse_inflow_ref[...], COARSE_SHAPE)
    coarse = walls_at_rest(coarse, flags, coarse_inflow, out_rows, out_cols)
    coarse = advance_at_rest(coarse, coarse_coef, coarse_step)

    rows_out = pair_matrix((out_rows, tile_rows), 0, None)
    cols_out = pair_matrix((tile_cols, out_cols), 1, None)
    paired = matmul(
        rows_out, jnp.concatenate([values[:tile_rows, :tile_cols] for values in state], axis=1)
    )
    stacked = jnp.concatenate(
        [paired[:, field * tile_cols: (field + 1) * tile_cols] for field in range(3)], axis=0
    )
    means = matmul(stacked, cols_out)
    for field in range(3):
        mean = means[field * out_rows: (field + 1) * out_rows] * 0.25
        mean_ref[field] = mean
        corr_ref[field] = mean - coarse[field][:out_rows, :out_cols]


EDGE_REACH = 32


def edge_kernel(
    flags_ref, noise_ref, fine_inflow_ref, coarse_inflow_ref, main_mean_ref, main_corr_ref,
    mean_ref, corr_ref,
):
    flags = [flags_ref[i] for i in range(4)]
    fine_rows = FINE_SHAPE[0]
    coarse_rows = COARSE_SHAPE[0]
    out_rows, out_cols = mean_ref.shape[1], mean_ref.shape[2]
    tile_rows = 2 * out_rows
    lanes = noise_ref.shape[2]
    half = lanes // 2
    fine_coef = noise_ref[0]
    noise_height = noise_ref[1]
    depth = 1.0 + 0.1 * noise_height
    state = (depth, 0.5 * depth, jnp.zeros_like(depth))
    fine_inflow = jnp.broadcast_to(fine_inflow_ref[...], fine_coef.shape)
    fine_left, fine_right = EDGE_REACH - 1, half + EDGE_REACH
    state = walls_at_rest(state, flags, fine_inflow, tile_rows, fine_right, fine_left)
    state = advance_at_rest(state, fine_coef, fine_step)
    state = apply_walls(state, flags, fine_inflow, tile_rows, fine_right, fine_left)
    state = advance(state, fine_coef, fine_step)

    rows_sum = pair_matrix((coarse_rows, fine_rows), 0, fine_rows - 2)
    cols_sum = pair_matrix((lanes, lanes), 1, None)
    paired = matmul(rows_sum, jnp.concatenate([fine_coef, noise_height], axis=1))
    small = matmul(jnp.concatenate([paired[:, :lanes], paired[:, lanes:]], axis=0), cols_sum)
    coarse_coef = small[:coarse_rows] * 0.25
    depth = 1.0 + 0.1 * (small[coarse_rows:] * 0.25)
    coarse = (depth, 0.5 * depth, jnp.zeros_like(depth))
    coarse_inflow = jnp.broadcast_to(coarse_inflow_ref[...], depth.shape)
    coarse_left, coarse_right = EDGE_REACH // 2 - 1, half // 2 + EDGE_REACH // 2
    coarse = walls_at_rest(coarse, flags, coarse_inflow, out_rows, coarse_right, coarse_left)
    coarse = advance_at_rest(coarse, coarse_coef, coarse_step)

    rows_out = pair_matrix((out_rows, tile_rows), 0, None)
    paired = matmul(
        rows_out, jnp.concatenate([values[:tile_rows, :] for values in state], axis=1)
    )
    stacked = jnp.concatenate(
        [paired[:, field * lanes: (field + 1) * lanes] for field in range(3)], axis=0
    )
    means = matmul(stacked, cols_sum)
    lane_at = lax.broadcasted_iota(jnp.int32, (out_rows, lanes), 1)
    first, last = EDGE_REACH // 2, half // 2 + EDGE_REACH // 2 - 1

    def patched(edge_values, main_values):
        to_first = pltpu.roll(edge_values, (lanes - first) % lanes, 1)
        to_last = pltpu.roll(edge_values, (out_cols - 1 - last) % lanes, 1)
        return jnp.where(
            lane_at == 0, to_first, jnp.where(lane_at == out_cols - 1, to_last, main_values)
        )

    for field in range(3):
        mean = means[field * out_rows: (field + 1) * out_rows] * 0.25
        mean_ref[field] = patched(mean, main_mean_ref[field])
        corr_ref[field] = patched(mean - coarse[field][:out_rows, :], main_corr_ref[field])


def body(friction, height, inflow):
    strip = lax.axis_index("col") * lax.axis_size("level") + lax.axis_index("level")
    strips = lax.axis_size("col") * lax.axis_size("level")
    row_index = lax.axis_index("row")
    flags = jnp.stack(
        [row_index == 0, row_index == lax.axis_size("row") - 1, strip == 0, strip == strips - 1]
    ).astype(jnp.int32)
    tile_rows, tile_cols = friction.shape[1], friction.shape[2]
    out_rows, out_cols = tile_rows // 2, tile_cols // 2

    tall, west, east = with_halo(jnp.concatenate([friction, height], axis=0))
    fields = tall.shape[0]
    gap = jnp.zeros((fields, FINE_SHAPE[0], FINE_SHAPE[1] - tile_cols), tall.dtype)
    noise = jnp.concatenate([tall, gap], axis=2)
    pad = jnp.zeros((fields, FINE_SHAPE[0], EDGE_REACH - HALO), tall.dtype)
    packed = jnp.concatenate(
        [pad, west, tall[:, :, :EDGE_REACH], tall[:, :, tile_cols - EDGE_REACH:], east, pad],
        axis=2,
    )
    lead = FINE_SHAPE[0] - tile_rows - HALO
    fine_inflow = wrapped_rows(inflow, row_index * tile_rows, FINE_SHAPE[0], lead)
    lead = COARSE_SHAPE[0] - out_rows - 1
    coarse_inflow = wrapped_rows(pair_mean(inflow), row_index * out_rows, COARSE_SHAPE[0], lead)

    out = jax.ShapeDtypeStruct((3, out_rows, out_cols), jnp.float32)
    vmem = pl.BlockSpec(memory_space=pltpu.VMEM)
    mean, corr = pl.pallas_call(
        level_kernel,
        out_shape=(out, out),
        in_specs=[pl.BlockSpec(memory_space=pltpu.SMEM), vmem, vmem, vmem],
        out_specs=(vmem, vmem),
    )(flags, noise, fine_inflow, coarse_inflow)
    mean, corr = pl.pallas_call(
        edge_kernel,
        out_shape=(out, out),
        in_specs=[pl.BlockSpec(memory_space=pltpu.SMEM)] + [vmem] * 5,
        out_specs=(vmem, vmem),
    )(flags, packed, fine_inflow, coarse_inflow, mean, corr)
    return (mean[None], corr[None])


def solution(mesh):
    in_specs = (P("level", "row", "col"), P("level", "row", "col"), P())
    out_specs = (P("level", None, "row", "col"), P("level", None, "row", "col"))
    return jax.shard_map(body, mesh=mesh, in_specs=in_specs, out_specs=out_specs, check_vma=False)
```

```python
import jax
import jax.numpy as jnp
from jax import lax
from jax.experimental import pallas as pl
from jax.experimental.pallas import tpu as pltpu
from jax.sharding import PartitionSpec as P

step_ratio = 0.15
fine_step = 0.15
coarse_step = 0.3
HALO = 2
FINE_SHAPE = (72, 384)
COARSE_SHAPE = (40, 256)


def pair_mean(values):
    paired = values.reshape(-1, 2)
    return (paired[:, 0] + paired[:, 1]) * 0.5


def swap_pairs(count, parity, place=lambda i: i):
    pairs = []
    for i in range(parity, count - 1, 2):
        pairs += [(place(i), place(i + 1)), (place(i + 1), place(i))]
    return pairs


def strip_place(strip):
    levels = lax.axis_size("level")
    return (strip % levels) * lax.axis_size("col") + strip // levels


def swapped(first, last, index, count, axis, place=lambda i: i):
    odd = index % 2 == 1
    got = []
    for parity in range(2):
        sends_last = odd if parity else jnp.logical_not(odd)
        block = jnp.where(sends_last, last, first)
        got.append(lax.ppermute(block, axis, swap_pairs(count, parity, place)))
    before = jnp.where(odd, got[0], got[1])
    after = jnp.where(odd, got[1], got[0])
    return before, after


def with_halo(noise):
    fields, count_rows, count_cols = noise.shape
    strips = lax.axis_size("col") * lax.axis_size("level")
    strip = lax.axis_index("col") * lax.axis_size("level") + lax.axis_index("level")
    rows = lax.axis_size("row")
    north, south = swapped(
        noise[:, :HALO], noise[:, -HALO:], lax.axis_index("row"), rows, "row"
    )
    gap_rows = FINE_SHAPE[0] - count_rows - 2 * HALO
    tall = jnp.concatenate(
        [noise, south, jnp.zeros((fields, gap_rows, count_cols), noise.dtype), north], axis=1
    )
    west, east = swapped(
        tall[:, :, :HALO], tall[:, :, -HALO:], strip, strips, ("level", "col"), strip_place
    )
    gap_cols = FINE_SHAPE[1] - count_cols - 2 * HALO
    return jnp.concatenate(
        [tall, east, jnp.zeros((fields, FINE_SHAPE[0], gap_cols), noise.dtype), west], axis=2
    )


def wrapped_rows(values, start, count, lead):
    padded = jnp.pad(values, lead)
    window = lax.dynamic_slice_in_dim(padded, start, count)
    return (0.5 + jnp.roll(window, -lead)).reshape(count, 1)


def next_of(values, axis):
    return pltpu.roll(values, values.shape[axis] - 1, axis)


def prev_of(values, axis):
    return pltpu.roll(values, 1, axis)


def apply_walls(state, flags, inflow_speed, bottom_row, right_col):
    depth, along_cols, along_rows = state
    shape = depth.shape
    row_at = lax.broadcasted_iota(jnp.int32, shape, 0)
    col_at = lax.broadcasted_iota(jnp.int32, shape, 1)
    top = jnp.logical_and(row_at == shape[0] - 1, flags[0] == 1)
    bottom = jnp.logical_and(row_at == bottom_row, flags[1] == 1)
    left = jnp.logical_and(col_at == shape[1] - 1, flags[2] == 1)
    right = jnp.logical_and(col_at == right_col, flags[3] == 1)

    def rows_fixed(values, sign):
        below = next_of(values, 0)
        above = prev_of(values, 0)
        if sign < 0:
            below = -below
            above = -above
        return jnp.where(top, below, jnp.where(bottom, above, values))

    depth = rows_fixed(depth, 1)
    along_cols = rows_fixed(along_cols, 1)
    along_rows = rows_fixed(along_rows, -1)
    source = next_of(depth, 1)
    entering = (source, source * inflow_speed, jnp.zeros_like(source))
    fixed = []
    for values, inflowing in zip((depth, along_cols, along_rows), entering):
        fixed.append(jnp.where(left, inflowing, jnp.where(right, prev_of(values, 1), values)))
    return tuple(fixed)


def face_flux(state, flux, speed, axis):
    reach = 0.5 * jnp.maximum(next_of(speed, axis), speed)
    return [
        0.5 * (next_of(f, axis) + f) - reach * (next_of(u, axis) - u)
        for f, u in zip(flux, state)
    ]


def advance(state, friction_coef, step):
    depth, along_cols, along_rows = state
    inverse = 1.0 / depth
    velocity = along_cols * inverse
    flux = (along_cols, along_cols * velocity + 0.5 * depth * depth, along_rows * velocity)
    face_x = face_flux(state, flux, jnp.abs(velocity) + jnp.sqrt(depth), 1)
    velocity = along_rows * inverse
    flux = (along_rows, along_cols * velocity, along_rows * velocity + 0.5 * depth * depth)
    face_y = face_flux(state, flux, jnp.abs(velocity) + jnp.sqrt(depth), 0)
    moved = [
        u - step_ratio * (fx - prev_of(fx, 1) + (fy - prev_of(fy, 0)))
        for u, fx, fy in zip(state, face_x, face_y)
    ]
    depth = moved[0]
    inverse = 1.0 / depth
    speed = jnp.sqrt(moved[1] * moved[1] + moved[2] * moved[2]) * inverse
    damping = 1.0 / (1.0 + step * friction_coef * speed * inverse)
    return (depth, moved[1] * damping, moved[2] * damping)


def walls_at_rest(state, flags, inflow_speed, bottom_row, right_col):
    depth, along_cols, _ = state
    depth, along_cols, _ = apply_walls(
        (depth, along_cols, depth), flags, inflow_speed, bottom_row, right_col
    )
    return (depth, along_cols, jnp.zeros_like(depth))


def advance_at_rest(state, friction_coef, step):
    depth, along_cols, _ = state
    velocity = along_cols * (1.0 / depth)
    root = jnp.sqrt(depth)
    flux = (along_cols, along_cols * velocity + 0.5 * depth * depth)
    face_x = face_flux((depth, along_cols), flux, jnp.abs(velocity) + root, 1)
    reach = 0.5 * jnp.maximum(next_of(root, 0), root)
    face_y = [0.0 - reach * (next_of(u, 0) - u) for u in (depth, along_cols)]
    pressure = 0.5 * depth * depth
    pressure_face = 0.5 * (next_of(pressure, 0) + pressure)
    moved = [
        u - step_ratio * (fx - prev_of(fx, 1) + (fy - prev_of(fy, 0)))
        for u, fx, fy in zip((depth, along_cols), face_x, face_y)
    ]
    moved.append(0.0 - step_ratio * (pressure_face - prev_of(pressure_face, 0)))
    depth = moved[0]
    inverse = 1.0 / depth
    speed = jnp.sqrt(moved[1] * moved[1] + moved[2] * moved[2]) * inverse
    damping = 1.0 / (1.0 + step * friction_coef * speed * inverse)
    return (depth, moved[1] * damping, moved[2] * damping)


def pair_matrix(shape, out_axis, last_from):
    out_at = lax.broadcasted_iota(jnp.int32, shape, out_axis)
    in_at = lax.broadcasted_iota(jnp.int32, shape, 1 - out_axis)
    hit = jnp.right_shift(in_at, 1) == out_at
    if last_from is not None:
        last = shape[out_axis] - 1
        hit = jnp.logical_or(hit, jnp.logical_and(out_at == last, in_at >= last_from))
    return hit.astype(jnp.float32)


def matmul(a, b):
    return jnp.dot(a, b, precision=lax.Precision.HIGHEST, preferred_element_type=jnp.float32)


def boundary_flags():
    strip = lax.axis_index("col") * lax.axis_size("level") + lax.axis_index("level")
    strips = lax.axis_size("col") * lax.axis_size("level")
    row_index = lax.axis_index("row")
    edges = (row_index == 0, row_index == lax.axis_size("row") - 1, strip == 0, strip == strips - 1)
    return [edge.astype(jnp.int32) for edge in edges]


def level_kernel(noise_ref, fine_inflow_ref, coarse_inflow_ref, mean_ref, corr_ref):
    flags = boundary_flags()
    fine_rows, fine_cols = FINE_SHAPE
    coarse_rows, coarse_cols = COARSE_SHAPE
    out_rows, out_cols = mean_ref.shape[1], mean_ref.shape[2]
    tile_rows, tile_cols = 2 * out_rows, 2 * out_cols

    fine_coef = noise_ref[0]
    noise_height = noise_ref[1]
    depth = 1.0 + 0.1 * noise_height
    state = (depth, 0.5 * depth, jnp.zeros_like(depth))
    fine_inflow = jnp.broadcast_to(fine_inflow_ref[...], FINE_SHAPE)
    state = walls_at_rest(state, flags, fine_inflow, tile_rows, tile_cols)
    state = advance_at_rest(state, fine_coef, fine_step)
    state = apply_walls(state, flags, fine_inflow, tile_rows, tile_cols)
    state = advance(state, fine_coef, fine_step)

    rows_sum = pair_matrix((coarse_rows, fine_rows), 0, fine_rows - 2)
    cols_sum = pair_matrix((fine_cols, coarse_cols), 1, fine_cols - 2)
    paired = matmul(rows_sum, jnp.concatenate([fine_coef, noise_height], axis=1))
    small = matmul(jnp.concatenate([paired[:, :fine_cols], paired[:, fine_cols:]], axis=0), cols_sum)
    coarse_coef = small[:coarse_rows] * 0.25
    depth = 1.0 + 0.1 * (small[coarse_rows:] * 0.25)
    coarse = (depth, 0.5 * depth, jnp.zeros_like(depth))
    coarse_inflow = jnp.broadcast_to(coarse_inflow_ref[...], COARSE_SHAPE)
    coarse = walls_at_rest(coarse, flags, coarse_inflow, out_rows, out_cols)
    coarse = advance_at_rest(coarse, coarse_coef, coarse_step)

    rows_out = pair_matrix((out_rows, tile_rows), 0, None)
    cols_out = pair_matrix((tile_cols, out_cols), 1, None)
    paired = matmul(
        rows_out, jnp.concatenate([values[:tile_rows, :tile_cols] for values in state], axis=1)
    )
    stacked = jnp.concatenate(
        [paired[:, field * tile_cols: (field + 1) * tile_cols] for field in range(3)], axis=0
    )
    means = matmul(stacked, cols_out)
    for field in range(3):
        mean = means[field * out_rows: (field + 1) * out_rows] * 0.25
        mean_ref[field] = mean
        corr_ref[field] = mean - coarse[field][:out_rows, :out_cols]


def body(friction, height, inflow):
    row_index = lax.axis_index("row")
    tile_rows, tile_cols = friction.shape[1], friction.shape[2]
    out_rows, out_cols = tile_rows // 2, tile_cols // 2

    noise = with_halo(jnp.concatenate([friction, height], axis=0))
    lead = FINE_SHAPE[0] - tile_rows - HALO
    fine_inflow = wrapped_rows(inflow, row_index * tile_rows, FINE_SHAPE[0], lead)
    lead = COARSE_SHAPE[0] - out_rows - 1
    coarse_inflow = wrapped_rows(pair_mean(inflow), row_index * out_rows, COARSE_SHAPE[0], lead)

    out = jax.ShapeDtypeStruct((3, out_rows, out_cols), jnp.float32)
    vmem = pl.BlockSpec(memory_space=pltpu.VMEM)
    mean, corr = pl.pallas_call(
        level_kernel,
        out_shape=(out, out),
        in_specs=[vmem, vmem, vmem],
        out_specs=(vmem, vmem),
    )(noise, fine_inflow, coarse_inflow)
    return (mean[None], corr[None])


def solution(mesh):
    in_specs = (P("level", "row", "col"), P("level", "row", "col"), P())
    out_specs = (P("level", None, "row", "col"), P("level", None, "row", "col"))
    return jax.shard_map(body, mesh=mesh, in_specs=in_specs, out_specs=out_specs, check_vma=False)
```

```python
import jax
import jax.numpy as jnp
from jax import lax
from jax.experimental import pallas as pl
from jax.experimental.pallas import tpu as pltpu
from jax.sharding import PartitionSpec as P

step_ratio = 0.15
fine_step = 0.15
coarse_step = 0.3
HALO = 2
FINE_SHAPE = (72, 384)
COARSE_SHAPE = (40, 256)


def pair_mean(values):
    paired = values.reshape(-1, 2)
    return (paired[:, 0] + paired[:, 1]) * 0.5


def swap_pairs(count, parity, place=lambda i: i):
    pairs = []
    for i in range(parity, count - 1, 2):
        pairs += [(place(i), place(i + 1)), (place(i + 1), place(i))]
    return pairs


def strip_place(strip):
    levels = lax.axis_size("level")
    return (strip % levels) * lax.axis_size("col") + strip // levels


def swapped(first, last, index, count, axis, place=lambda i: i):
    odd = index % 2 == 1
    got = []
    for parity in range(2):
        sends_last = odd if parity else jnp.logical_not(odd)
        block = jnp.where(sends_last, last, first)
        got.append(lax.ppermute(block, axis, swap_pairs(count, parity, place)))
    before = jnp.where(odd, got[0], got[1])
    after = jnp.where(odd, got[1], got[0])
    return before, after


def with_halo(noise):
    fields, count_rows, count_cols = noise.shape
    strips = lax.axis_size("col") * lax.axis_size("level")
    strip = lax.axis_index("col") * lax.axis_size("level") + lax.axis_index("level")
    rows = lax.axis_size("row")
    north, south = swapped(
        noise[:, :HALO], noise[:, -HALO:], lax.axis_index("row"), rows, "row"
    )
    gap_rows = FINE_SHAPE[0] - count_rows - 2 * HALO
    tall = jnp.concatenate(
        [noise, south, jnp.zeros((fields, gap_rows, count_cols), noise.dtype), north], axis=1
    )
    west, east = swapped(
        tall[:, :, :HALO], tall[:, :, -HALO:], strip, strips, ("level", "col"), strip_place
    )
    gap_cols = FINE_SHAPE[1] - count_cols - 2 * HALO
    return jnp.concatenate(
        [tall, east, jnp.zeros((fields, FINE_SHAPE[0], gap_cols), noise.dtype), west], axis=2
    )


def wrapped_rows(values, start, count, lead):
    padded = jnp.pad(values, lead)
    window = lax.dynamic_slice_in_dim(padded, start, count)
    return (0.5 + jnp.roll(window, -lead)).reshape(count, 1)


def next_of(values, axis):
    return pltpu.roll(values, values.shape[axis] - 1, axis)


def prev_of(values, axis):
    return pltpu.roll(values, 1, axis)


def apply_walls(state, flags, inflow_speed, bottom_row, right_col):
    depth, along_cols, along_rows = state
    shape = depth.shape
    row_at = lax.broadcasted_iota(jnp.int32, shape, 0)
    col_at = lax.broadcasted_iota(jnp.int32, shape, 1)
    top = jnp.logical_and(row_at == shape[0] - 1, flags[0] == 1)
    bottom = jnp.logical_and(row_at == bottom_row, flags[1] == 1)
    left = jnp.logical_and(col_at == shape[1] - 1, flags[2] == 1)
    right = jnp.logical_and(col_at == right_col, flags[3] == 1)

    def rows_fixed(values, sign):
        below = next_of(values, 0)
        above = prev_of(values, 0)
        if sign < 0:
            below = -below
            above = -above
        return jnp.where(top, below, jnp.where(bottom, above, values))

    depth = rows_fixed(depth, 1)
    along_cols = rows_fixed(along_cols, 1)
    along_rows = rows_fixed(along_rows, -1)
    source = next_of(depth, 1)
    entering = (source, source * inflow_speed, jnp.zeros_like(source))
    fixed = []
    for values, inflowing in zip((depth, along_cols, along_rows), entering):
        fixed.append(jnp.where(left, inflowing, jnp.where(right, prev_of(values, 1), values)))
    return tuple(fixed)


def face_flux(state, flux, speed, axis):
    reach = 0.5 * jnp.maximum(next_of(speed, axis), speed)
    return [
        0.5 * (next_of(f, axis) + f) - reach * (next_of(u, axis) - u)
        for f, u in zip(flux, state)
    ]


def advance(state, friction_coef, step):
    depth, along_cols, along_rows = state
    inverse = 1.0 / depth
    velocity = along_cols * inverse
    flux = (along_cols, along_cols * velocity + 0.5 * depth * depth, along_rows * velocity)
    face_x = face_flux(state, flux, jnp.abs(velocity) + jnp.sqrt(depth), 1)
    velocity = along_rows * inverse
    flux = (along_rows, along_cols * velocity, along_rows * velocity + 0.5 * depth * depth)
    face_y = face_flux(state, flux, jnp.abs(velocity) + jnp.sqrt(depth), 0)
    moved = [
        u - step_ratio * (fx - prev_of(fx, 1) + (fy - prev_of(fy, 0)))
        for u, fx, fy in zip(state, face_x, face_y)
    ]
    depth = moved[0]
    inverse = 1.0 / depth
    speed = jnp.sqrt(moved[1] * moved[1] + moved[2] * moved[2]) * inverse
    damping = 1.0 / (1.0 + step * friction_coef * speed * inverse)
    return (depth, moved[1] * damping, moved[2] * damping)


def walls_at_rest(state, flags, inflow_speed, bottom_row, right_col):
    depth, along_cols, _ = state
    depth, along_cols, _ = apply_walls(
        (depth, along_cols, depth), flags, inflow_speed, bottom_row, right_col
    )
    return (depth, along_cols, jnp.zeros_like(depth))


def advance_at_rest(state, friction_coef, step):
    depth, along_cols, _ = state
    velocity = along_cols * (1.0 / depth)
    root = jnp.sqrt(depth)
    flux = (along_cols, along_cols * velocity + 0.5 * depth * depth)
    face_x = face_flux((depth, along_cols), flux, jnp.abs(velocity) + root, 1)
    reach = 0.5 * jnp.maximum(next_of(root, 0), root)
    face_y = [0.0 - reach * (next_of(u, 0) - u) for u in (depth, along_cols)]
    pressure = 0.5 * depth * depth
    pressure_face = 0.5 * (next_of(pressure, 0) + pressure)
    moved = [
        u - step_ratio * (fx - prev_of(fx, 1) + (fy - prev_of(fy, 0)))
        for u, fx, fy in zip((depth, along_cols), face_x, face_y)
    ]
    moved.append(0.0 - step_ratio * (pressure_face - prev_of(pressure_face, 0)))
    depth = moved[0]
    inverse = 1.0 / depth
    speed = jnp.sqrt(moved[1] * moved[1] + moved[2] * moved[2]) * inverse
    damping = 1.0 / (1.0 + step * friction_coef * speed * inverse)
    return (depth, moved[1] * damping, moved[2] * damping)


def pair_matrix(shape, out_axis, last_from):
    out_at = lax.broadcasted_iota(jnp.int32, shape, out_axis)
    in_at = lax.broadcasted_iota(jnp.int32, shape, 1 - out_axis)
    hit = jnp.right_shift(in_at, 1) == out_at
    if last_from is not None:
        last = shape[out_axis] - 1
        hit = jnp.logical_or(hit, jnp.logical_and(out_at == last, in_at >= last_from))
    return hit.astype(jnp.float32)


def pair_sum(pairs, values, pairs_first):
    pairs = pairs.astype(jnp.bfloat16)
    total = None
    rest = values
    for _ in range(3):
        part = rest.astype(jnp.bfloat16)
        rest = rest - part.astype(jnp.float32)
        operands = (pairs, part) if pairs_first else (part, pairs)
        product = jnp.dot(*operands, preferred_element_type=jnp.float32)
        total = product if total is None else total + product
    return total


def boundary_flags():
    strip = lax.axis_index("col") * lax.axis_size("level") + lax.axis_index("level")
    strips = lax.axis_size("col") * lax.axis_size("level")
    row_index = lax.axis_index("row")
    edges = (row_index == 0, row_index == lax.axis_size("row") - 1, strip == 0, strip == strips - 1)
    return [edge.astype(jnp.int32) for edge in edges]


def level_kernel(noise_ref, fine_inflow_ref, coarse_inflow_ref, mean_ref, corr_ref):
    flags = boundary_flags()
    fine_rows, fine_cols = FINE_SHAPE
    coarse_rows, coarse_cols = COARSE_SHAPE
    out_rows, out_cols = mean_ref.shape[1], mean_ref.shape[2]
    tile_rows, tile_cols = 2 * out_rows, 2 * out_cols

    fine_coef = noise_ref[0]
    noise_height = noise_ref[1]
    depth = 1.0 + 0.1 * noise_height
    state = (depth, 0.5 * depth, jnp.zeros_like(depth))
    fine_inflow = jnp.broadcast_to(fine_inflow_ref[...], FINE_SHAPE)
    state = walls_at_rest(state, flags, fine_inflow, tile_rows, tile_cols)
    state = advance_at_rest(state, fine_coef, fine_step)
    state = apply_walls(state, flags, fine_inflow, tile_rows, tile_cols)
    state = advance(state, fine_coef, fine_step)

    rows_sum = pair_matrix((coarse_rows, fine_rows), 0, fine_rows - 2)
    cols_sum = pair_matrix((fine_cols, coarse_cols), 1, fine_cols - 2)
    paired = pair_sum(rows_sum, jnp.concatenate([fine_coef, noise_height], axis=1), True)
    small = pair_sum(
        cols_sum, jnp.concatenate([paired[:, :fine_cols], paired[:, fine_cols:]], axis=0), False
    )
    coarse_coef = small[:coarse_rows] * 0.25
    depth = 1.0 + 0.1 * (small[coarse_rows:] * 0.25)
    coarse = (depth, 0.5 * depth, jnp.zeros_like(depth))
    coarse_inflow = jnp.broadcast_to(coarse_inflow_ref[...], COARSE_SHAPE)
    coarse = walls_at_rest(coarse, flags, coarse_inflow, out_rows, out_cols)
    coarse = advance_at_rest(coarse, coarse_coef, coarse_step)

    rows_out = pair_matrix((out_rows, tile_rows), 0, None)
    cols_out = pair_matrix((tile_cols, out_cols), 1, None)
    paired = pair_sum(
        rows_out,
        jnp.concatenate([values[:tile_rows, :tile_cols] for values in state], axis=1),
        True,
    )
    stacked = jnp.concatenate(
        [paired[:, field * tile_cols: (field + 1) * tile_cols] for field in range(3)], axis=0
    )
    means = pair_sum(cols_out, stacked, False)
    for field in range(3):
        mean = means[field * out_rows: (field + 1) * out_rows] * 0.25
        mean_ref[field] = mean
        corr_ref[field] = mean - coarse[field][:out_rows, :out_cols]


def body(friction, height, inflow):
    row_index = lax.axis_index("row")
    tile_rows, tile_cols = friction.shape[1], friction.shape[2]
    out_rows, out_cols = tile_rows // 2, tile_cols // 2

    noise = with_halo(jnp.concatenate([friction, height], axis=0))
    lead = FINE_SHAPE[0] - tile_rows - HALO
    fine_inflow = wrapped_rows(inflow, row_index * tile_rows, FINE_SHAPE[0], lead)
    lead = COARSE_SHAPE[0] - out_rows - 1
    coarse_inflow = wrapped_rows(pair_mean(inflow), row_index * out_rows, COARSE_SHAPE[0], lead)

    out = jax.ShapeDtypeStruct((3, out_rows, out_cols), jnp.float32)
    vmem = pl.BlockSpec(memory_space=pltpu.VMEM)
    mean, corr = pl.pallas_call(
        level_kernel,
        out_shape=(out, out),
        in_specs=[vmem, vmem, vmem],
        out_specs=(vmem, vmem),
    )(noise, fine_inflow, coarse_inflow)
    return (mean[None], corr[None])


def solution(mesh):
    in_specs = (P("level", "row", "col"), P("level", "row", "col"), P())
    out_specs = (P("level", None, "row", "col"), P("level", None, "row", "col"))
    return jax.shard_map(body, mesh=mesh, in_specs=in_specs, out_specs=out_specs, check_vma=False)
```

```python
import jax
import jax.numpy as jnp
from jax import lax
from jax.experimental import pallas as pl
from jax.experimental.pallas import tpu as pltpu
from jax.sharding import PartitionSpec as P

step_ratio = 0.15
fine_step = 0.15
coarse_step = 0.3
HALO = 2
FINE_SHAPE = (72, 384)
COARSE_SHAPE = (40, 256)


def pair_mean(values):
    paired = values.reshape(-1, 2)
    return (paired[:, 0] + paired[:, 1]) * 0.5


def swap_pairs(count, parity, place=lambda i: i):
    pairs = []
    for i in range(parity, count - 1, 2):
        pairs += [(place(i), place(i + 1)), (place(i + 1), place(i))]
    return pairs


def strip_place(strip):
    levels = lax.axis_size("level")
    return (strip % levels) * lax.axis_size("col") + strip // levels


def swapped(first, last, index, count, axis, place=lambda i: i):
    odd = index % 2 == 1
    got = []
    for parity in range(2):
        sends_last = odd if parity else jnp.logical_not(odd)
        block = jnp.where(sends_last, last, first)
        got.append(lax.ppermute(block, axis, swap_pairs(count, parity, place)))
    before = jnp.where(odd, got[0], got[1])
    after = jnp.where(odd, got[1], got[0])
    return before, after


def with_halo(noise):
    fields, count_rows, count_cols = noise.shape
    strips = lax.axis_size("col") * lax.axis_size("level")
    strip = lax.axis_index("col") * lax.axis_size("level") + lax.axis_index("level")
    rows = lax.axis_size("row")
    north, south = swapped(
        noise[:, :HALO], noise[:, -HALO:], lax.axis_index("row"), rows, "row"
    )
    gap_rows = FINE_SHAPE[0] - count_rows - 2 * HALO
    tall = jnp.concatenate(
        [noise, south, jnp.zeros((fields, gap_rows, count_cols), noise.dtype), north], axis=1
    )
    west, east = swapped(
        tall[:, :, :HALO], tall[:, :, -HALO:], strip, strips, ("level", "col"), strip_place
    )
    gap_cols = FINE_SHAPE[1] - count_cols - 2 * HALO
    return jnp.concatenate(
        [tall, east, jnp.zeros((fields, FINE_SHAPE[0], gap_cols), noise.dtype), west], axis=2
    )


def wrapped_rows(values, start, count, lead):
    padded = jnp.pad(values, lead)
    window = lax.dynamic_slice_in_dim(padded, start, count)
    return (0.5 + jnp.roll(window, -lead)).reshape(count, 1)


def next_of(values, axis):
    return pltpu.roll(values, values.shape[axis] - 1, axis)


def prev_of(values, axis):
    return pltpu.roll(values, 1, axis)


def apply_walls(state, flags, inflow_speed, bottom_row, right_col):
    depth, along_cols, along_rows = state
    shape = depth.shape
    row_at = lax.broadcasted_iota(jnp.int32, shape, 0)
    col_at = lax.broadcasted_iota(jnp.int32, shape, 1)
    top = jnp.logical_and(row_at == shape[0] - 1, flags[0] == 1)
    bottom = jnp.logical_and(row_at == bottom_row, flags[1] == 1)
    left = jnp.logical_and(col_at == shape[1] - 1, flags[2] == 1)
    right = jnp.logical_and(col_at == right_col, flags[3] == 1)

    def rows_fixed(values, sign):
        below = next_of(values, 0)
        above = prev_of(values, 0)
        if sign < 0:
            below = -below
            above = -above
        return jnp.where(top, below, jnp.where(bottom, above, values))

    depth = rows_fixed(depth, 1)
    along_cols = rows_fixed(along_cols, 1)
    along_rows = rows_fixed(along_rows, -1)
    source = next_of(depth, 1)
    entering = (source, source * inflow_speed, jnp.zeros_like(source))
    fixed = []
    for values, inflowing in zip((depth, along_cols, along_rows), entering):
        fixed.append(jnp.where(left, inflowing, jnp.where(right, prev_of(values, 1), values)))
    return tuple(fixed)


def face_flux(state, flux, speed, axis):
    reach = 0.5 * jnp.maximum(next_of(speed, axis), speed)
    return [
        0.5 * (next_of(f, axis) + f) - reach * (next_of(u, axis) - u)
        for f, u in zip(flux, state)
    ]


def advance(state, friction_coef, step):
    depth, along_cols, along_rows = state
    inverse = 1.0 / depth
    velocity = along_cols * inverse
    flux = (along_cols, along_cols * velocity + 0.5 * depth * depth, along_rows * velocity)
    face_x = face_flux(state, flux, jnp.abs(velocity) + jnp.sqrt(depth), 1)
    velocity = along_rows * inverse
    flux = (along_rows, along_cols * velocity, along_rows * velocity + 0.5 * depth * depth)
    face_y = face_flux(state, flux, jnp.abs(velocity) + jnp.sqrt(depth), 0)
    moved = [
        u - step_ratio * (fx - prev_of(fx, 1) + (fy - prev_of(fy, 0)))
        for u, fx, fy in zip(state, face_x, face_y)
    ]
    depth = moved[0]
    inverse = 1.0 / depth
    speed = jnp.sqrt(moved[1] * moved[1] + moved[2] * moved[2]) * inverse
    damping = 1.0 / (1.0 + step * friction_coef * speed * inverse)
    return (depth, moved[1] * damping, moved[2] * damping)


def walls_at_rest(state, flags, inflow_speed, bottom_row, right_col):
    depth, along_cols, _ = state
    depth, along_cols, _ = apply_walls(
        (depth, along_cols, depth), flags, inflow_speed, bottom_row, right_col
    )
    return (depth, along_cols, jnp.zeros_like(depth))


def advance_at_rest(state, friction_coef, step):
    depth, along_cols, _ = state
    velocity = along_cols * (1.0 / depth)
    root = jnp.sqrt(depth)
    flux = (along_cols, along_cols * velocity + 0.5 * depth * depth)
    face_x = face_flux((depth, along_cols), flux, jnp.abs(velocity) + root, 1)
    reach = 0.5 * jnp.maximum(next_of(root, 0), root)
    face_y = [0.0 - reach * (next_of(u, 0) - u) for u in (depth, along_cols)]
    pressure = 0.5 * depth * depth
    pressure_face = 0.5 * (next_of(pressure, 0) + pressure)
    moved = [
        u - step_ratio * (fx - prev_of(fx, 1) + (fy - prev_of(fy, 0)))
        for u, fx, fy in zip((depth, along_cols), face_x, face_y)
    ]
    moved.append(0.0 - step_ratio * (pressure_face - prev_of(pressure_face, 0)))
    depth = moved[0]
    inverse = 1.0 / depth
    speed = jnp.sqrt(moved[1] * moved[1] + moved[2] * moved[2]) * inverse
    damping = 1.0 / (1.0 + step * friction_coef * speed * inverse)
    return (depth, moved[1] * damping, moved[2] * damping)


def pair_matrix(shape, out_axis, last_from):
    out_at = lax.broadcasted_iota(jnp.int32, shape, out_axis)
    in_at = lax.broadcasted_iota(jnp.int32, shape, 1 - out_axis)
    hit = jnp.right_shift(in_at, 1) == out_at
    if last_from is not None:
        last = shape[out_axis] - 1
        hit = jnp.logical_or(hit, jnp.logical_and(out_at == last, in_at >= last_from))
    return hit.astype(jnp.float32)


def pair_sum(pairs, values, pairs_first):
    pairs = pairs.astype(jnp.bfloat16)
    total = None
    rest = values
    for _ in range(3):
        part = rest.astype(jnp.bfloat16)
        rest = rest - part.astype(jnp.float32)
        operands = (pairs, part) if pairs_first else (part, pairs)
        product = jnp.dot(*operands, preferred_element_type=jnp.float32)
        total = product if total is None else total + product
    return total


def boundary_flags():
    strip = lax.axis_index("col") * lax.axis_size("level") + lax.axis_index("level")
    strips = lax.axis_size("col") * lax.axis_size("level")
    row_index = lax.axis_index("row")
    edges = (row_index == 0, row_index == lax.axis_size("row") - 1, strip == 0, strip == strips - 1)
    return [edge.astype(jnp.int32) for edge in edges]


def level_kernel(noise_ref, inflow_ref, mean_ref, corr_ref):
    flags = boundary_flags()
    fine_rows, fine_cols = FINE_SHAPE
    coarse_rows, coarse_cols = COARSE_SHAPE
    out_rows, out_cols = mean_ref.shape[1], mean_ref.shape[2]
    tile_rows, tile_cols = 2 * out_rows, 2 * out_cols

    fine_coef = noise_ref[0]
    noise_height = noise_ref[1]
    depth = 1.0 + 0.1 * noise_height
    state = (depth, 0.5 * depth, jnp.zeros_like(depth))
    fine_inflow = jnp.broadcast_to(inflow_ref[: FINE_SHAPE[0]], FINE_SHAPE)
    state = walls_at_rest(state, flags, fine_inflow, tile_rows, tile_cols)
    state = advance_at_rest(state, fine_coef, fine_step)
    state = apply_walls(state, flags, fine_inflow, tile_rows, tile_cols)
    state = advance(state, fine_coef, fine_step)

    rows_sum = pair_matrix((coarse_rows, fine_rows), 0, fine_rows - 2)
    cols_sum = pair_matrix((fine_cols, coarse_cols), 1, fine_cols - 2)
    paired = pair_sum(rows_sum, jnp.concatenate([fine_coef, noise_height], axis=1), True)
    small = pair_sum(
        cols_sum, jnp.concatenate([paired[:, :fine_cols], paired[:, fine_cols:]], axis=0), False
    )
    coarse_coef = small[:coarse_rows] * 0.25
    depth = 1.0 + 0.1 * (small[coarse_rows:] * 0.25)
    coarse = (depth, 0.5 * depth, jnp.zeros_like(depth))
    coarse_inflow = jnp.broadcast_to(inflow_ref[FINE_SHAPE[0]:], COARSE_SHAPE)
    coarse = walls_at_rest(coarse, flags, coarse_inflow, out_rows, out_cols)
    coarse = advance_at_rest(coarse, coarse_coef, coarse_step)

    rows_out = pair_matrix((out_rows, tile_rows), 0, None)
    cols_out = pair_matrix((tile_cols, out_cols), 1, None)
    paired = pair_sum(
        rows_out,
        jnp.concatenate([values[:tile_rows, :tile_cols] for values in state], axis=1),
        True,
    )
    stacked = jnp.concatenate(
        [paired[:, field * tile_cols: (field + 1) * tile_cols] for field in range(3)], axis=0
    )
    means = pair_sum(cols_out, stacked, False)
    for field in range(3):
        mean = means[field * out_rows: (field + 1) * out_rows] * 0.25
        mean_ref[field] = mean
        corr_ref[field] = mean - coarse[field][:out_rows, :out_cols]


def body(friction, height, inflow):
    row_index = lax.axis_index("row")
    tile_rows, tile_cols = friction.shape[1], friction.shape[2]
    out_rows, out_cols = tile_rows // 2, tile_cols // 2

    noise = with_halo(jnp.concatenate([friction, height], axis=0))
    lead = FINE_SHAPE[0] - tile_rows - HALO
    fine_inflow = wrapped_rows(inflow, row_index * tile_rows, FINE_SHAPE[0], lead)
    lead = COARSE_SHAPE[0] - out_rows - 1
    coarse_inflow = wrapped_rows(pair_mean(inflow), row_index * out_rows, COARSE_SHAPE[0], lead)

    out = jax.ShapeDtypeStruct((3, out_rows, out_cols), jnp.float32)
    vmem = pl.BlockSpec(memory_space=pltpu.VMEM)
    mean, corr = pl.pallas_call(
        level_kernel,
        out_shape=(out, out),
        in_specs=[vmem, vmem],
        out_specs=(vmem, vmem),
    )(noise, jnp.concatenate([fine_inflow, coarse_inflow], axis=0))
    return (mean[None], corr[None])


def solution(mesh):
    in_specs = (P("level", "row", "col"), P("level", "row", "col"), P())
    out_specs = (P("level", None, "row", "col"), P("level", None, "row", "col"))
    return jax.shard_map(body, mesh=mesh, in_specs=in_specs, out_specs=out_specs, check_vma=False)
```
